512 devices in a mesh: row: 32 (over z, x), col: 16 (over y, core).
Axes of the slice: x: 4, y: 8, z: 8, core: 2. Of those that a mesh axis runs over, the one named last changes fastest.
Arguments:
- tokens: bfloat16 [16384, 5376], P('row', 'col'), may hold values from -240 to 240
- gain: float32 [5376], P('col'), may hold values from 0.1 to 1.9
- query_gain: float32 [128], replicated, may hold values from 0.1 to 1.9
- key_gain: float32 [128], replicated, may hold values from 0.1 to 1.9
- w_query: bfloat16 [5376, 4096], P('row', 'col'), may hold values from -0.21808224 to 0.21808224
- w_key: bfloat16 [5376, 2048], P('row', 'col'), may hold values from -0.21808224 to 0.21808224
- w_value: bfloat16 [5376, 2048], P('row', 'col'), may hold values from -0.21808224 to 0.21808224
Outputs:
- attended: bfloat16 [16384, 4096], P('row', 'col')
The draws below stay inside these ranges and needn't reach their ends.
All inputs are finite; a program needn't handle non-finite values.
Results may differ from the reference program's by a relative error of at most 0.022.
Values may be sent and summed in bfloat16 or wider, within the bound.
No kernel may reach another device: no remote copies, remote signals or barrier semaphores. Data moves between devices by JAX's collectives and lax.ppermute only.
A program may use at most 64 MiB of HBM per device.

```python
import math
import jax
import jax.numpy as jnp
from jax import lax

D = 5376
H = 32
KVH = 16
HD = 128
WINDOW = 1024
TOKENS = 16384


def draw_panel(key, columns):
    first, second = jax.random.split(key, 2)
    base = jnp.clip(jax.random.normal(first, (D, columns), jnp.float32), -5.0, 5.0)
    ramp = jnp.exp(math.log(10.0) * jnp.arange(D, dtype=jnp.float32) / max(D - 1, 1))
    rough = jax.random.uniform(second, (D, 1), jnp.float32, 0.7, 1.4)
    return base * ramp[:, None] * rough / math.sqrt(22.0 * D)


def draw_w_query(key, part):
    return draw_panel(jax.random.fold_in(key, 11), H * HD).astype(jnp.bfloat16)


def draw_w_key(key, part):
    return draw_panel(jax.random.fold_in(key, 12), KVH * HD).astype(jnp.bfloat16)


def draw_w_value(key, part):
    return draw_panel(jax.random.fold_in(key, 13), KVH * HD).astype(jnp.bfloat16)


def draw_tokens(key, part):
    first, second, third = jax.random.split(jax.random.fold_in(key, 14), 3)
    base = jnp.clip(jax.random.normal(first, (TOKENS, D), jnp.float32), -5.0, 5.0)
    row_scale = jnp.exp(jax.random.uniform(second, (TOKENS, 1), jnp.float32, 0.0, math.log(10.0)))
    ramp = jnp.exp(math.log(3.0) * jnp.arange(D, dtype=jnp.float32) / max(D - 1, 1))
    rough = jax.random.uniform(third, (D,), jnp.float32, 0.6, 1.6)
    return (base * row_scale * (ramp * rough)[None, :]).astype(jnp.bfloat16)


def setup_inputs(seed: int = 0) -> dict:
    splits = jax.random.split(jax.random.key(seed), 8)
    return {
        "tokens": draw_tokens(jax.random.fold_in(splits[7], 71), 0),
        "gain": jnp.clip(1.0 + 0.18 * jax.random.normal(splits[1], (D,), jnp.float32), 0.1, 1.9),
        "query_gain": jnp.clip(1.0 + 0.18 * jax.random.normal(splits[2], (HD,), jnp.float32), 0.1, 1.9),
        "key_gain": jnp.clip(1.0 + 0.18 * jax.random.normal(splits[3], (HD,), jnp.float32), 0.1, 1.9),
        "w_query": draw_w_query(jax.random.fold_in(splits[7], 71), 0),
        "w_key": draw_w_key(jax.random.fold_in(splits[7], 71), 0),
        "w_value": draw_w_value(jax.random.fold_in(splits[7], 71), 0),
    }


EPS = 1e-06
CLIP_FRACTION = 0.25
QUERY_SCALAR = 168.0
ROPE_BASE = 10000.0

def clip_columns(weight):
    widened = weight.astype(jnp.float32)
    largest = lax.optimization_barrier(jnp.max(jnp.abs(widened), axis=0))
    bound = CLIP_FRACTION * largest
    return jnp.clip(widened, -bound, bound).astype(jnp.bfloat16)

def head_norm(values, head_gain):
    return values * lax.rsqrt(lax.optimization_barrier(jnp.mean(values * values, axis=-1, keepdims=True)) + EPS) * head_gain

def rotate(values, positions):
    half = values.shape[-1] // 2
    freqs = ROPE_BASE ** (-(jnp.arange(half, dtype=jnp.float32) * 2.0 / values.shape[-1]))
    angles = positions.astype(jnp.float32)[:, None] * freqs[None, :]
    cosine = jnp.cos(angles)[:, None, :]
    sine = jnp.sin(angles)[:, None, :]
    first = values[..., :half]
    second = values[..., half:]
    return jnp.concatenate([first * cosine - second * sine, second * cosine + first * sine], axis=-1)

def reference(tokens, gain, query_gain, key_gain, w_query, w_key, w_value):
    widened = tokens.astype(jnp.float32)
    inverse = lax.rsqrt(lax.optimization_barrier(jnp.mean(widened * widened, axis=1, keepdims=True)) + EPS)
    normed = (widened * inverse * gain[None, :]).astype(jnp.bfloat16)
    positions = jnp.arange(TOKENS, dtype=jnp.int32)
    query = jnp.dot(normed, clip_columns(w_query), preferred_element_type=jnp.float32).reshape(TOKENS, H, HD)
    keys = jnp.dot(normed, clip_columns(w_key), preferred_element_type=jnp.float32).reshape(TOKENS, KVH, HD)
    values = jnp.dot(normed, clip_columns(w_value), preferred_element_type=jnp.float32).reshape(TOKENS, KVH, HD)
    query = rotate(head_norm(query, query_gain), positions).astype(jnp.bfloat16)
    keys = rotate(head_norm(keys, key_gain), positions).astype(jnp.bfloat16)
    values = values.astype(jnp.bfloat16)
    padding = jnp.zeros((WINDOW, KVH, HD), jnp.bfloat16)
    keys_pad = jnp.concatenate([padding, keys], axis=0)
    values_pad = jnp.concatenate([padding, values], axis=0)
    group = H // KVH
    scale = QUERY_SCALAR ** (-0.5)

    def attend(block):
        start = (block * WINDOW).astype(jnp.int32)
        block_query = lax.dynamic_slice_in_dim(query, start, WINDOW, 0).astype(jnp.float32).reshape(WINDOW, KVH, group, HD)
        block_keys = lax.dynamic_slice_in_dim(keys_pad, start, 2 * WINDOW, 0).astype(jnp.float32)
        block_values = lax.dynamic_slice_in_dim(values_pad, start, 2 * WINDOW, 0).astype(jnp.float32)
        scores = jnp.einsum('tkgd,skd->kgts', block_query, block_keys) * scale
        query_pos = start + jnp.arange(WINDOW, dtype=jnp.int32)
        key_pos = start - WINDOW + jnp.arange(2 * WINDOW, dtype=jnp.int32)
        distance = query_pos[:, None] - key_pos[None, :]
        allowed = (distance >= 0) & (distance < WINDOW) & (key_pos[None, :] >= 0)
        expo = jnp.where(allowed, jnp.exp(scores), 0.0)
        total = lax.optimization_barrier(jnp.sum(expo, axis=-1, keepdims=True))
        probs = (expo / total).astype(jnp.bfloat16)
        probs = lax.optimization_barrier(probs).astype(jnp.float32)
        output = jnp.einsum('kgts,skd->tkgd', probs, block_values)
        return output.reshape(WINDOW, H * HD).astype(jnp.bfloat16)
    blocks = lax.map(attend, jnp.arange(TOKENS // WINDOW, dtype=jnp.int32))
    return blocks.reshape(TOKENS, H * HD)
```

```python
import jax
import jax.numpy as jnp
from jax import lax
from jax.sharding import PartitionSpec as P

D = 5376
HD = 128
WINDOW = 1024


EPS = 1e-06
CLIP_FRACTION = 0.25
QUERY_SCALAR = 168.0
ROPE_BASE = 10000.0


def shifted(array, axis, by):
    peers = lax.axis_size(axis)
    pairs = [(i, i + by) for i in range(peers) if 0 <= i + by < peers]
    return lax.ppermute(array, axis, pairs)


def clip_with(weight, largest):
    bound = CLIP_FRACTION * largest
    return jnp.clip(weight.astype(jnp.float32), -bound, bound).astype(jnp.bfloat16)


def column_max(weight):
    return jnp.max(jnp.abs(weight.astype(jnp.float32)), axis=0)


def head_norm(values, head_gain):
    return values * lax.rsqrt(jnp.mean(values * values, axis=-1, keepdims=True) + EPS) * head_gain


def rotate(values, positions):
    half = values.shape[-1] // 2
    freqs = ROPE_BASE ** (-(jnp.arange(half, dtype=jnp.float32) * 2.0 / values.shape[-1]))
    angles = positions.astype(jnp.float32)[:, None] * freqs[None, :]
    cosine = jnp.cos(angles)[:, None, :]
    sine = jnp.sin(angles)[:, None, :]
    first = values[..., :half]
    second = values[..., half:]
    return jnp.concatenate(
        [first * cosine - second * sine, second * cosine + first * sine], axis=-1
    )


def local(tokens, gain, query_gain, key_gain, w_query, w_key, w_value):
    rows = tokens.shape[0]
    query_cols = w_query.shape[1]
    key_cols = w_key.shape[1]
    stacked = jnp.concatenate([w_query, w_key, w_value], axis=1)
    panel = lax.all_gather(stacked, "row", axis=0, tiled=True)
    clipped = clip_with(panel, column_max(panel))
    widened = tokens.astype(jnp.float32)
    squares = lax.psum(jnp.sum(widened * widened, axis=1), "col")
    inverse = lax.rsqrt(squares / D + EPS)[:, None]
    normed = (widened * inverse * gain[None, :]).astype(jnp.bfloat16)
    whole = lax.all_gather(normed, "col", axis=1, tiled=True)
    projected = jnp.dot(whole, clipped, preferred_element_type=jnp.float32)
    query = projected[:, :query_cols]
    keys = projected[:, query_cols : query_cols + key_cols]
    values = projected[:, query_cols + key_cols :]
    heads_local = query_cols // HD
    kv_local = key_cols // HD
    group = heads_local // kv_local
    positions = lax.axis_index("row") * rows + jnp.arange(rows, dtype=jnp.int32)
    query = rotate(head_norm(query.reshape(rows, heads_local, HD), query_gain), positions).astype(
        jnp.bfloat16
    )
    keys = rotate(head_norm(keys.reshape(rows, kv_local, HD), key_gain), positions).astype(
        jnp.bfloat16
    )
    values = values.reshape(rows, kv_local, HD).astype(jnp.bfloat16)
    blocks_back = WINDOW // rows
    earlier_keys = []
    earlier_values = []
    for offset in range(blocks_back, 0, -1):
        moved_keys, moved_values = shifted((keys, values), "row", offset)
        earlier_keys.append(moved_keys)
        earlier_values.append(moved_values)
    all_keys = jnp.concatenate(earlier_keys + [keys], axis=0)
    all_values = jnp.concatenate(earlier_values + [values], axis=0)
    key_pos = (
        positions[0] - blocks_back * rows + jnp.arange((blocks_back + 1) * rows, dtype=jnp.int32)
    )
    grouped = query.reshape(rows, kv_local, group, HD)
    scores = jnp.einsum(
        "tkgd,skd->kgts", grouped, all_keys, preferred_element_type=jnp.float32
    ) * QUERY_SCALAR ** (-0.5)
    distance = positions[:, None] - key_pos[None, :]
    allowed = (distance >= 0) & (distance < WINDOW) & (key_pos[None, :] >= 0)
    expo = jnp.where(allowed, jnp.exp(scores), 0.0)
    total = jnp.sum(expo, axis=-1, keepdims=True)
    probs = (expo / total).astype(jnp.bfloat16)
    output = jnp.einsum("kgts,skd->tkgd", probs, all_values, preferred_element_type=jnp.float32)
    return output.reshape(rows, query_cols).astype(jnp.bfloat16)


def solution(mesh):
    placed = (
        P("row", "col"),
        P("col"),
        P(),
        P(),
        P("row", "col"),
        P("row", "col"),
        P("row", "col"),
    )
    return jax.shard_map(
        local, mesh=mesh, in_specs=placed, out_specs=P("row", "col"), check_vma=False
    )
```

```python
import jax
import jax.numpy as jnp
from jax import lax
from jax.sharding import Mesh, PartitionSpec as P

D = 5376
HD = 128
WINDOW = 1024


EPS = 1e-06
CLIP_FRACTION = 0.25
QUERY_SCALAR = 168.0
ROPE_BASE = 10000.0


def shifted(array, axis, by):
    peers = lax.axis_size(axis)
    pairs = [(i, i + by) for i in range(peers) if 0 <= i + by < peers]
    return lax.ppermute(array, axis, pairs)


def ring_gather(parts, axis, dims):
    peers = lax.axis_size(axis)
    right = [(i, (i + 1) % peers) for i in range(peers)]
    left = [(i, (i - 1) % peers) for i in range(peers)]
    held = {0: parts}
    forward = parts
    backward = parts
    for step in range(1, peers // 2 + 1):
        forward = lax.ppermute(forward, axis, right)
        held[peers - step] = forward
        if step < peers - step:
            backward = lax.ppermute(backward, axis, left)
            held[step] = backward
    start = (peers - lax.axis_index(axis)) % peers
    out = []
    for leaf, (dim) in enumerate(dims):
        stacked = jnp.concatenate([held[k][leaf] for k in range(peers)], axis=dim)
        doubled = jnp.concatenate([stacked, stacked], axis=dim)
        size = parts[leaf].shape[dim]
        out.append(lax.dynamic_slice_in_dim(doubled, start * size, peers * size, dim))
    return tuple(out)


def clip_with(weight, largest):
    bound = CLIP_FRACTION * largest
    return jnp.clip(weight.astype(jnp.float32), -bound, bound).astype(jnp.bfloat16)


def column_max(weight):
    return jnp.max(jnp.abs(weight.astype(jnp.float32)), axis=0)


def head_norm(values, head_gain):
    return values * lax.rsqrt(jnp.mean(values * values, axis=-1, keepdims=True) + EPS) * head_gain


def rotate(values, positions):
    half = values.shape[-1] // 2
    freqs = ROPE_BASE ** (-(jnp.arange(half, dtype=jnp.float32) * 2.0 / values.shape[-1]))
    angles = positions.astype(jnp.float32)[:, None] * freqs[None, :]
    cosine = jnp.cos(angles)[:, None, :]
    sine = jnp.sin(angles)[:, None, :]
    first = values[..., :half]
    second = values[..., half:]
    return jnp.concatenate(
        [first * cosine - second * sine, second * cosine + first * sine], axis=-1
    )


def local(tokens, gain, query_gain, key_gain, w_query, w_key, w_value):
    rows = tokens.shape[0]
    query_cols = w_query.shape[1]
    key_cols = w_key.shape[1]
    stacked = jnp.concatenate([w_query, w_key, w_value], axis=1)
    panel = lax.all_gather(stacked, "row", axis=0, tiled=True)
    clipped = clip_with(panel, column_max(panel))
    rows_tokens, piece = tokens.shape
    cores = lax.axis_size("cc")
    along_y, gain_y = ring_gather((tokens, gain), "cy", (1, 0))
    along_all, gain_all = ring_gather((along_y, gain_y), "cc", (1, 0))
    blocks = along_all.shape[1] // (cores * piece)
    full = (
        along_all.reshape(rows_tokens, cores, blocks, piece)
        .transpose(0, 2, 1, 3)
        .reshape(rows_tokens, cores * blocks * piece)
    )
    full_gain = gain_all.reshape(cores, blocks, piece).transpose(1, 0, 2).reshape(-1)
    widened = full.astype(jnp.float32)
    squares = jnp.sum(widened * widened, axis=1)
    inverse = lax.rsqrt(squares / D + EPS)[:, None]
    whole = (widened * inverse * full_gain[None, :]).astype(jnp.bfloat16)
    projected = jnp.dot(whole, clipped, preferred_element_type=jnp.float32)
    query = projected[:, :query_cols]
    keys = projected[:, query_cols : query_cols + key_cols]
    values = projected[:, query_cols + key_cols :]
    heads_local = query_cols // HD
    kv_local = key_cols // HD
    group = heads_local // kv_local
    positions = lax.axis_index("row") * rows + jnp.arange(rows, dtype=jnp.int32)
    query = rotate(head_norm(query.reshape(rows, heads_local, HD), query_gain), positions).astype(
        jnp.bfloat16
    )
    keys = rotate(head_norm(keys.reshape(rows, kv_local, HD), key_gain), positions).astype(
        jnp.bfloat16
    )
    values = values.reshape(rows, kv_local, HD).astype(jnp.bfloat16)
    blocks_back = WINDOW // rows
    both = jnp.concatenate([keys, values], axis=1)
    earlier = [shifted(both, "row", offset) for offset in range(blocks_back, 0, -1)]
    joined = jnp.concatenate(earlier + [both], axis=0)
    all_keys = joined[:, :kv_local]
    all_values = joined[:, kv_local:]
    key_pos = (
        positions[0] - blocks_back * rows + jnp.arange((blocks_back + 1) * rows, dtype=jnp.int32)
    )
    grouped = query.reshape(rows, kv_local, group, HD)
    scores = jnp.einsum(
        "tkgd,skd->kgts", grouped, all_keys, preferred_element_type=jnp.float32
    ) * QUERY_SCALAR ** (-0.5)
    distance = positions[:, None] - key_pos[None, :]
    allowed = (distance >= 0) & (distance < WINDOW) & (key_pos[None, :] >= 0)
    expo = jnp.where(allowed, jnp.exp(scores), 0.0)
    total = jnp.sum(expo, axis=-1, keepdims=True)
    probs = (expo / total).astype(jnp.bfloat16)
    output = jnp.einsum("kgts,skd->tkgd", probs, all_values, preferred_element_type=jnp.float32)
    return output.reshape(rows, query_cols).astype(jnp.bfloat16)


CORES_PER_CHIP = 2


def solution(mesh):
    rows, cols = mesh.shape["row"], mesh.shape["col"]
    split = Mesh(
        mesh.devices.reshape(rows, cols // CORES_PER_CHIP, CORES_PER_CHIP), ("row", "cy", "cc")
    )
    col = ("cy", "cc")
    placed = (
        P("row", col),
        P(col),
        P(),
        P(),
        P("row", col),
        P("row", col),
        P("row", col),
    )
    return jax.shard_map(
        local, mesh=split, in_specs=placed, out_specs=P("row", col), check_vma=False
    )
```

```python
import jax
import jax.numpy as jnp
from jax import lax
from jax.sharding import Mesh, PartitionSpec as P

D = 5376
HD = 128
WINDOW = 1024


EPS = 1e-06
CLIP_FRACTION = 0.25
QUERY_SCALAR = 168.0
ROPE_BASE = 10000.0


def shifted(array, axis, by):
    peers = lax.axis_size(axis)
    pairs = [(i, i + by) for i in range(peers) if 0 <= i + by < peers]
    return lax.ppermute(array, axis, pairs)


def ring_gather(parts, axis, dims):
    peers = lax.axis_size(axis)
    right = [(i, (i + 1) % peers) for i in range(peers)]
    left = [(i, (i - 1) % peers) for i in range(peers)]
    held = {0: parts}
    forward = parts
    backward = parts
    for step in range(1, peers // 2 + 1):
        forward = lax.ppermute(forward, axis, right)
        held[peers - step] = forward
        if step < peers - step:
            backward = lax.ppermute(backward, axis, left)
            held[step] = backward
    start = (peers - lax.axis_index(axis)) % peers
    out = []
    for leaf, (dim) in enumerate(dims):
        stacked = jnp.concatenate([held[k][leaf] for k in range(peers)], axis=dim)
        doubled = jnp.concatenate([stacked, stacked], axis=dim)
        size = parts[leaf].shape[dim]
        out.append(lax.dynamic_slice_in_dim(doubled, start * size, peers * size, dim))
    return tuple(out)


def clip_with(weight, largest):
    bound = CLIP_FRACTION * largest
    return jnp.clip(weight.astype(jnp.float32), -bound, bound).astype(jnp.bfloat16)


def column_max(weight):
    return jnp.max(jnp.abs(weight.astype(jnp.float32)), axis=0)


def head_norm(values, head_gain):
    return values * lax.rsqrt(jnp.mean(values * values, axis=-1, keepdims=True) + EPS) * head_gain


def rotate(values, positions):
    half = values.shape[-1] // 2
    freqs = ROPE_BASE ** (-(jnp.arange(half, dtype=jnp.float32) * 2.0 / values.shape[-1]))
    angles = positions.astype(jnp.float32)[:, None] * freqs[None, :]
    cosine = jnp.cos(angles)[:, None, :]
    sine = jnp.sin(angles)[:, None, :]
    first = values[..., :half]
    second = values[..., half:]
    return jnp.concatenate(
        [first * cosine - second * sine, second * cosine + first * sine], axis=-1
    )


def local(tokens, gain, query_gain, key_gain, w_query, w_key, w_value):
    rows = tokens.shape[0]
    query_cols = w_query.shape[1]
    key_cols = w_key.shape[1]
    stacked = jnp.concatenate([w_query, w_key, w_value], axis=1)
    panel = lax.all_gather(stacked, "row", axis=0, tiled=True)
    clipped = clip_with(panel, column_max(panel))
    rows_tokens, piece = tokens.shape
    cores = lax.axis_size("cc")
    high = gain.astype(jnp.bfloat16)
    rest = gain - high.astype(jnp.float32)
    middle = rest.astype(jnp.bfloat16)
    low = (rest - middle.astype(jnp.float32)).astype(jnp.bfloat16)
    filler = jnp.zeros((GAIN_ROWS - 3, piece), jnp.bfloat16)
    packed = jnp.concatenate([tokens, high[None], middle[None], low[None], filler], axis=0)
    (along_y,) = ring_gather((packed,), "cy", (1,))
    (along_all,) = ring_gather((along_y,), "cc", (1,))
    blocks = along_all.shape[1] // (cores * piece)
    split = along_all[rows_tokens : rows_tokens + 3].astype(jnp.float32)
    full_gain = split[0] + (split[1] + split[2])
    widened = along_all[:rows_tokens].astype(jnp.float32)
    squares = jnp.sum(widened * widened, axis=1)
    inverse = lax.rsqrt(squares / D + EPS)[:, None]
    whole = (widened * inverse * full_gain[None, :]).astype(jnp.bfloat16)
    ordered = (
        clipped.reshape(blocks, cores, piece, clipped.shape[1])
        .transpose(1, 0, 2, 3)
        .reshape(clipped.shape)
    )
    kv_part = jnp.dot(whole, ordered[:, query_cols:], preferred_element_type=jnp.float32)
    keys = kv_part[:, :key_cols]
    values = kv_part[:, key_cols:]
    query = jnp.dot(whole, ordered[:, :query_cols], preferred_element_type=jnp.float32)
    heads_local = query_cols // HD
    kv_local = key_cols // HD
    group = heads_local // kv_local
    positions = lax.axis_index("row") * rows + jnp.arange(rows, dtype=jnp.int32)
    query = rotate(head_norm(query.reshape(rows, heads_local, HD), query_gain), positions).astype(
        jnp.bfloat16
    )
    keys = rotate(head_norm(keys.reshape(rows, kv_local, HD), key_gain), positions).astype(
        jnp.bfloat16
    )
    values = values.reshape(rows, kv_local, HD).astype(jnp.bfloat16)
    blocks_back = WINDOW // rows
    both = jnp.concatenate([keys, values], axis=1)
    earlier = [shifted(both, "row", offset) for offset in range(blocks_back, 0, -1)]
    joined = jnp.concatenate(earlier + [both], axis=0)
    all_keys = joined[:, :kv_local]
    all_values = joined[:, kv_local:]
    key_pos = (
        positions[0] - blocks_back * rows + jnp.arange((blocks_back + 1) * rows, dtype=jnp.int32)
    )
    grouped = query.reshape(rows, kv_local, group, HD)
    scores = jnp.einsum(
        "tkgd,skd->kgts", grouped, all_keys, preferred_element_type=jnp.float32
    ) * QUERY_SCALAR ** (-0.5)
    distance = positions[:, None] - key_pos[None, :]
    allowed = (distance >= 0) & (distance < WINDOW) & (key_pos[None, :] >= 0)
    expo = jnp.where(allowed, jnp.exp(scores), 0.0)
    total = jnp.sum(expo, axis=-1, keepdims=True)
    probs = (expo / total).astype(jnp.bfloat16)
    output = jnp.einsum("kgts,skd->tkgd", probs, all_values, preferred_element_type=jnp.float32)
    return output.reshape(rows, query_cols).astype(jnp.bfloat16)


CORES_PER_CHIP = 2
GAIN_ROWS = 8


def solution(mesh):
    rows, cols = mesh.shape["row"], mesh.shape["col"]
    split = Mesh(
        mesh.devices.reshape(rows, cols // CORES_PER_CHIP, CORES_PER_CHIP), ("row", "cy", "cc")
    )
    col = ("cy", "cc")
    placed = (
        P("row", col),
        P(col),
        P(),
        P(),
        P("row", col),
        P("row", col),
        P("row", col),
    )
    return jax.shard_map(
        local, mesh=split, in_specs=placed, out_specs=P("row", col), check_vma=False
    )
```

```python
import jax
import jax.numpy as jnp
from jax import lax
from jax.sharding import Mesh, PartitionSpec as P

D = 5376
HD = 128
WINDOW = 1024


EPS = 1e-06
CLIP_FRACTION = 0.25
QUERY_SCALAR = 168.0
ROPE_BASE = 10000.0


def shifted(array, axis, by):
    peers = lax.axis_size(axis)
    pairs = [(i, i + by) for i in range(peers) if 0 <= i + by < peers]
    return lax.ppermute(array, axis, pairs)


def ring_gather(parts, axis, dims):
    peers = lax.axis_size(axis)
    right = [(i, (i + 1) % peers) for i in range(peers)]
    left = [(i, (i - 1) % peers) for i in range(peers)]
    held = {0: parts}
    forward = parts
    backward = parts
    for step in range(1, peers // 2 + 1):
        forward = lax.ppermute(forward, axis, right)
        held[peers - step] = forward
        if step < peers - step:
            backward = lax.ppermute(backward, axis, left)
            held[step] = backward
    start = (peers - lax.axis_index(axis)) % peers
    out = []
    for leaf, (dim) in enumerate(dims):
        stacked = jnp.concatenate([held[k][leaf] for k in range(peers)], axis=dim)
        doubled = jnp.concatenate([stacked, stacked], axis=dim)
        size = parts[leaf].shape[dim]
        out.append(lax.dynamic_slice_in_dim(doubled, start * size, peers * size, dim))
    return tuple(out)


def clip_with(weight, largest):
    bound = CLIP_FRACTION * largest
    return jnp.clip(weight.astype(jnp.float32), -bound, bound).astype(jnp.bfloat16)


def column_max(weight):
    return jnp.max(jnp.abs(weight.astype(jnp.float32)), axis=0)


def head_norm(values, head_gain):
    return values * lax.rsqrt(jnp.mean(values * values, axis=-1, keepdims=True) + EPS) * head_gain


def rotate(values, positions):
    half = values.shape[-1] // 2
    freqs = ROPE_BASE ** (-(jnp.arange(half, dtype=jnp.float32) * 2.0 / values.shape[-1]))
    angles = positions.astype(jnp.float32)[:, None] * freqs[None, :]
    cosine = jnp.cos(angles)[:, None, :]
    sine = jnp.sin(angles)[:, None, :]
    first = values[..., :half]
    second = values[..., half:]
    return jnp.concatenate(
        [first * cosine - second * sine, second * cosine + first * sine], axis=-1
    )


def local(tokens, gain, query_gain, key_gain, w_query, w_key, w_value):
    rows = tokens.shape[0]
    query_cols = w_query.shape[1]
    key_cols = w_key.shape[1]
    stacked = jnp.concatenate([w_query, w_key, w_value], axis=1)
    weight_rows = stacked.shape[0]
    aligned = -(-weight_rows // TILE_ROWS) * TILE_ROWS
    padded = jnp.pad(stacked, ((0, aligned - weight_rows), (0, 0)))
    slabs = lax.all_gather(padded, "row", axis=0, tiled=True)
    panel = slabs.reshape(-1, aligned, stacked.shape[1])[:, :weight_rows].reshape(-1, stacked.shape[1])
    clipped = clip_with(panel, column_max(panel))
    rows_tokens, piece = tokens.shape
    cores = lax.axis_size("cc")
    high = gain.astype(jnp.bfloat16)
    rest = gain - high.astype(jnp.float32)
    middle = rest.astype(jnp.bfloat16)
    low = (rest - middle.astype(jnp.float32)).astype(jnp.bfloat16)
    filler = jnp.zeros((GAIN_ROWS - 3, piece), jnp.bfloat16)
    packed = jnp.concatenate([tokens, high[None], middle[None], low[None], filler], axis=0)
    (along_y,) = ring_gather((packed,), "cy", (1,))
    (along_all,) = ring_gather((along_y,), "cc", (1,))
    blocks = along_all.shape[1] // (cores * piece)
    split = along_all[rows_tokens : rows_tokens + 3].astype(jnp.float32)
    full_gain = split[0] + (split[1] + split[2])
    widened = along_all[:rows_tokens].astype(jnp.float32)
    squares = jnp.sum(widened * widened, axis=1)
    inverse = lax.rsqrt(squares / D + EPS)[:, None]
    whole = (widened * inverse * full_gain[None, :]).astype(jnp.bfloat16)
    ordered = (
        clipped.reshape(blocks, cores, piece, clipped.shape[1])
        .transpose(1, 0, 2, 3)
        .reshape(clipped.shape)
    )
    kv_part = jnp.dot(whole, ordered[:, query_cols:], preferred_element_type=jnp.float32)
    keys = kv_part[:, :key_cols]
    values = kv_part[:, key_cols:]
    query = jnp.dot(whole, ordered[:, :query_cols], preferred_element_type=jnp.float32)
    heads_local = query_cols // HD
    kv_local = key_cols // HD
    group = heads_local // kv_local
    positions = lax.axis_index("row") * rows + jnp.arange(rows, dtype=jnp.int32)
    query = rotate(head_norm(query.reshape(rows, heads_local, HD), query_gain), positions).astype(
        jnp.bfloat16
    )
    keys = rotate(head_norm(keys.reshape(rows, kv_local, HD), key_gain), positions).astype(
        jnp.bfloat16
    )
    values = values.reshape(rows, kv_local, HD).astype(jnp.bfloat16)
    blocks_back = WINDOW // rows
    both = jnp.concatenate([keys, values], axis=1)
    earlier = [shifted(both, "row", offset) for offset in range(blocks_back, 0, -1)]
    joined = jnp.concatenate(earlier + [both], axis=0)
    all_keys = joined[:, :kv_local]
    all_values = joined[:, kv_local:]
    key_pos = (
        positions[0] - blocks_back * rows + jnp.arange((blocks_back + 1) * rows, dtype=jnp.int32)
    )
    grouped = query.reshape(rows, kv_local, group, HD)
    scores = jnp.einsum(
        "tkgd,skd->kgts", grouped, all_keys, preferred_element_type=jnp.float32
    ) * QUERY_SCALAR ** (-0.5)
    distance = positions[:, None] - key_pos[None, :]
    allowed = (distance >= 0) & (distance < WINDOW) & (key_pos[None, :] >= 0)
    expo = jnp.where(allowed, jnp.exp(scores), 0.0)
    total = jnp.sum(expo, axis=-1, keepdims=True)
    probs = (expo / total).astype(jnp.bfloat16)
    output = jnp.einsum("kgts,skd->tkgd", probs, all_values, preferred_element_type=jnp.float32)
    return output.reshape(rows, query_cols).astype(jnp.bfloat16)


CORES_PER_CHIP = 2
GAIN_ROWS = 8
TILE_ROWS = 16


def solution(mesh):
    rows, cols = mesh.shape["row"], mesh.shape["col"]
    split = Mesh(
        mesh.devices.reshape(rows, cols // CORES_PER_CHIP, CORES_PER_CHIP), ("row", "cy", "cc")
    )
    col = ("cy", "cc")
    placed = (
        P("row", col),
        P(col),
        P(),
        P(),
        P("row", col),
        P("row", col),
        P("row", col),
    )
    return jax.shard_map(
        local, mesh=split, in_specs=placed, out_specs=P("row", col), check_vma=False
    )
```

```python
import jax
import jax.numpy as jnp
from jax import lax
from jax.sharding import Mesh, PartitionSpec as P

D = 5376
HD = 128
WINDOW = 1024


EPS = 1e-06
CLIP_FRACTION = 0.25
QUERY_SCALAR = 168.0
ROPE_BASE = 10000.0


ROW = ("rz", "rx")


def shifted(array, axis, by):
    peers = lax.axis_size(axis)
    pairs = [(i, i + by) for i in range(peers) if 0 <= i + by < peers]
    return lax.ppermute(array, axis, pairs)


def ring_gather(parts, axis, dims):
    peers = lax.axis_size(axis)
    right = [(i, (i + 1) % peers) for i in range(peers)]
    left = [(i, (i - 1) % peers) for i in range(peers)]
    held = {0: parts}
    forward = parts
    backward = parts
    for step in range(1, peers // 2 + 1):
        forward = lax.ppermute(forward, axis, right)
        held[peers - step] = forward
        if step < peers - step:
            backward = lax.ppermute(backward, axis, left)
            held[step] = backward
    start = (peers - lax.axis_index(axis)) % peers
    out = []
    for leaf, (dim) in enumerate(dims):
        stacked = jnp.concatenate([held[k][leaf] for k in range(peers)], axis=dim)
        doubled = jnp.concatenate([stacked, stacked], axis=dim)
        size = parts[leaf].shape[dim]
        out.append(lax.dynamic_slice_in_dim(doubled, start * size, peers * size, dim))
    return tuple(out)


def clip_with(weight, largest):
    bound = CLIP_FRACTION * largest
    return jnp.clip(weight.astype(jnp.float32), -bound, bound).astype(jnp.bfloat16)


def column_max(weight):
    return jnp.max(jnp.abs(weight.astype(jnp.float32)), axis=0)


def head_norm(values, head_gain):
    return values * lax.rsqrt(jnp.mean(values * values, axis=-1, keepdims=True) + EPS) * head_gain


def rotate(values, positions):
    half = values.shape[-1] // 2
    freqs = ROPE_BASE ** (-(jnp.arange(half, dtype=jnp.float32) * 2.0 / values.shape[-1]))
    angles = positions.astype(jnp.float32)[:, None] * freqs[None, :]
    cosine = jnp.cos(angles)[:, None, :]
    sine = jnp.sin(angles)[:, None, :]
    first = values[..., :half]
    second = values[..., half:]
    return jnp.concatenate(
        [first * cosine - second * sine, second * cosine + first * sine], axis=-1
    )


def local(tokens, gain, query_gain, key_gain, w_query, w_key, w_value):
    rows = tokens.shape[0]
    query_cols = w_query.shape[1]
    key_cols = w_key.shape[1]
    stacked = jnp.concatenate([w_query, w_key, w_value], axis=1)
    weight_rows, weight_cols = stacked.shape
    aligned = -(-(weight_rows + 1) // TILE_ROWS) * TILE_ROWS
    local_max = jnp.max(jnp.abs(stacked), axis=0)
    padded = jnp.concatenate(
        [
            stacked,
            local_max[None],
            jnp.zeros((aligned - weight_rows - 1, weight_cols), stacked.dtype),
        ],
        axis=0,
    )
    slabs = lax.all_gather(padded, ROW, axis=0, tiled=True).reshape(-1, aligned, weight_cols)
    largest = jnp.max(slabs[:, weight_rows].astype(jnp.float32), axis=0)
    clipped = clip_with(slabs[:, :weight_rows].reshape(-1, weight_cols), largest)
    rows_tokens, piece = tokens.shape
    cores = lax.axis_size("cc")
    high = gain.astype(jnp.bfloat16)
    rest = gain - high.astype(jnp.float32)
    middle = rest.astype(jnp.bfloat16)
    low = (rest - middle.astype(jnp.float32)).astype(jnp.bfloat16)
    filler = jnp.zeros((GAIN_ROWS - 3, piece), jnp.bfloat16)
    packed = jnp.concatenate([tokens, high[None], middle[None], low[None], filler], axis=0)
    (along_y,) = ring_gather((packed,), "cy", (1,))
    (along_all,) = ring_gather((along_y,), "cc", (1,))
    blocks = along_all.shape[1] // (cores * piece)
    split = along_all[rows_tokens : rows_tokens + 3].astype(jnp.float32)
    full_gain = split[0] + (split[1] + split[2])
    widened = along_all[:rows_tokens].astype(jnp.float32)
    squares = jnp.sum(widened * widened, axis=1)
    inverse = lax.rsqrt(squares / D + EPS)[:, None]
    whole = (widened * inverse * full_gain[None, :]).astype(jnp.bfloat16)
    ordered = (
        clipped.reshape(blocks, cores, piece, clipped.shape[1])
        .transpose(1, 0, 2, 3)
        .reshape(clipped.shape)
    )
    kv_part = jnp.dot(whole, ordered[:, query_cols:], preferred_element_type=jnp.float32)
    keys = kv_part[:, :key_cols]
    values = kv_part[:, key_cols:]
    query = jnp.dot(whole, ordered[:, :query_cols], preferred_element_type=jnp.float32)
    heads_local = query_cols // HD
    kv_local = key_cols // HD
    group = heads_local // kv_local
    positions = lax.axis_index(ROW) * rows + jnp.arange(rows, dtype=jnp.int32)
    query = rotate(head_norm(query.reshape(rows, heads_local, HD), query_gain), positions).astype(
        jnp.bfloat16
    )
    keys = rotate(head_norm(keys.reshape(rows, kv_local, HD), key_gain), positions).astype(
        jnp.bfloat16
    )
    values = values.reshape(rows, kv_local, HD).astype(jnp.bfloat16)
    blocks_back = WINDOW // rows
    both = jnp.concatenate([keys, values], axis=1)
    earlier = [shifted(both, ROW, offset) for offset in range(blocks_back, 0, -1)]
    joined = jnp.concatenate(earlier + [both], axis=0)
    all_keys = joined[:, :kv_local]
    all_values = joined[:, kv_local:]
    key_pos = (
        positions[0] - blocks_back * rows + jnp.arange((blocks_back + 1) * rows, dtype=jnp.int32)
    )
    grouped = query.reshape(rows, kv_local, group, HD)
    scores = jnp.einsum(
        "tkgd,skd->kgts", grouped, all_keys, preferred_element_type=jnp.float32
    ) * QUERY_SCALAR ** (-0.5)
    distance = positions[:, None] - key_pos[None, :]
    allowed = (distance >= 0) & (distance < WINDOW) & (key_pos[None, :] >= 0)
    expo = jnp.where(allowed, jnp.exp(scores), 0.0)
    total = jnp.sum(expo, axis=-1, keepdims=True)
    probs = (expo / total).astype(jnp.bfloat16)
    output = jnp.einsum("kgts,skd->tkgd", probs, all_values, preferred_element_type=jnp.float32)
    return output.reshape(rows, query_cols).astype(jnp.bfloat16)


CORES_PER_CHIP = 2
GAIN_ROWS = 8
TILE_ROWS = 16


def solution(mesh):
    rows, cols = mesh.shape["row"], mesh.shape["col"]
    minor = len({tuple(getattr(d, "coords", (0,)))[0] for d in mesh.devices[:, 0].flat})
    if rows % minor:
        minor = 1
    split = Mesh(
        mesh.devices.reshape(rows // minor, minor, cols // CORES_PER_CHIP, CORES_PER_CHIP),
        ("rz", "rx", "cy", "cc"),
    )
    col = ("cy", "cc")
    placed = (
        P(ROW, col),
        P(col),
        P(),
        P(),
        P(ROW, col),
        P(ROW, col),
        P(ROW, col),
    )
    return jax.shard_map(
        local, mesh=split, in_specs=placed, out_specs=P(ROW, col), check_vma=False
    )
```

```python
import jax
import jax.numpy as jnp
from jax import lax
from jax.sharding import Mesh, PartitionSpec as P

D = 5376
HD = 128
WINDOW = 1024


EPS = 1e-06
CLIP_FRACTION = 0.25
QUERY_SCALAR = 168.0
ROPE_BASE = 10000.0


ROW = ("rz", "rx")


def shifted(array, axis, by):
    peers = lax.axis_size(axis)
    pairs = [(i, i + by) for i in range(peers) if 0 <= i + by < peers]
    return lax.ppermute(array, axis, pairs)


def ring_gather(parts, axis, dims):
    peers = lax.axis_size(axis)
    right = [(i, (i + 1) % peers) for i in range(peers)]
    left = [(i, (i - 1) % peers) for i in range(peers)]
    held = {0: parts}
    forward = parts
    backward = parts
    for step in range(1, peers // 2 + 1):
        forward = lax.ppermute(forward, axis, right)
        held[peers - step] = forward
        if step < peers - step:
            backward = lax.ppermute(backward, axis, left)
            held[step] = backward
    start = (peers - lax.axis_index(axis)) % peers
    out = []
    for leaf, (dim) in enumerate(dims):
        stacked = jnp.concatenate([held[k][leaf] for k in range(peers)], axis=dim)
        doubled = jnp.concatenate([stacked, stacked], axis=dim)
        size = parts[leaf].shape[dim]
        out.append(lax.dynamic_slice_in_dim(doubled, start * size, peers * size, dim))
    return tuple(out)


def clip_with(weight, largest):
    bound = CLIP_FRACTION * largest
    return jnp.clip(weight.astype(jnp.float32), -bound, bound).astype(jnp.bfloat16)


def column_max(weight):
    return jnp.max(jnp.abs(weight.astype(jnp.float32)), axis=0)


def head_norm(values, head_gain):
    return values * lax.rsqrt(jnp.mean(values * values, axis=-1, keepdims=True) + EPS) * head_gain


def rotate(values, positions):
    half = values.shape[-1] // 2
    freqs = ROPE_BASE ** (-(jnp.arange(half, dtype=jnp.float32) * 2.0 / values.shape[-1]))
    angles = positions.astype(jnp.float32)[:, None] * freqs[None, :]
    cosine = jnp.cos(angles)[:, None, :]
    sine = jnp.sin(angles)[:, None, :]
    first = values[..., :half]
    second = values[..., half:]
    return jnp.concatenate(
        [first * cosine - second * sine, second * cosine + first * sine], axis=-1
    )


def local(tokens, gain, query_gain, key_gain, w_query, w_key, w_value):
    rows = tokens.shape[0]
    query_cols = w_query.shape[1]
    key_cols = w_key.shape[1]
    stacked = jnp.concatenate([w_query, w_key, w_value], axis=1)
    weight_rows, weight_cols = stacked.shape
    aligned = -(-(weight_rows + 1) // TILE_ROWS) * TILE_ROWS
    local_max = jnp.max(jnp.abs(stacked), axis=0)
    padded = jnp.concatenate(
        [
            stacked,
            local_max[None],
            jnp.zeros((aligned - weight_rows - 1, weight_cols), stacked.dtype),
        ],
        axis=0,
    )
    (along_x,) = ring_gather((padded,), "rx", (0,))
    (gathered,) = ring_gather((along_x,), "rz", (0,))
    slabs = gathered.reshape(-1, aligned, weight_cols)
    largest = jnp.max(slabs[:, weight_rows].astype(jnp.float32), axis=0)
    clipped = clip_with(slabs[:, :weight_rows].reshape(-1, weight_cols), largest)
    rows_tokens, piece = tokens.shape
    cores = lax.axis_size("cc")
    high = gain.astype(jnp.bfloat16)
    rest = gain - high.astype(jnp.float32)
    middle = rest.astype(jnp.bfloat16)
    low = (rest - middle.astype(jnp.float32)).astype(jnp.bfloat16)
    filler = jnp.zeros((GAIN_ROWS - 3, piece), jnp.bfloat16)
    packed = jnp.concatenate([tokens, high[None], middle[None], low[None], filler], axis=0)
    along_all = lax.all_gather(packed, ("cy", "cc"), axis=1, tiled=True)
    split = along_all[rows_tokens : rows_tokens + 3].astype(jnp.float32)
    full_gain = split[0] + (split[1] + split[2])
    widened = along_all[:rows_tokens].astype(jnp.float32)
    squares = jnp.sum(widened * widened, axis=1)
    inverse = lax.rsqrt(squares / D + EPS)[:, None]
    whole = (widened * inverse * full_gain[None, :]).astype(jnp.bfloat16)
    ordered = clipped
    kv_part = jnp.dot(whole, ordered[:, query_cols:], preferred_element_type=jnp.float32)
    keys = kv_part[:, :key_cols]
    values = kv_part[:, key_cols:]
    query = jnp.dot(whole, ordered[:, :query_cols], preferred_element_type=jnp.float32)
    heads_local = query_cols // HD
    kv_local = key_cols // HD
    group = heads_local // kv_local
    positions = lax.axis_index(ROW) * rows + jnp.arange(rows, dtype=jnp.int32)
    query = rotate(head_norm(query.reshape(rows, heads_local, HD), query_gain), positions).astype(
        jnp.bfloat16
    )
    keys = rotate(head_norm(keys.reshape(rows, kv_local, HD), key_gain), positions).astype(
        jnp.bfloat16
    )
    values = values.reshape(rows, kv_local, HD).astype(jnp.bfloat16)
    blocks_back = WINDOW // rows
    both = jnp.concatenate([keys, values], axis=1)
    earlier = [shifted(both, ROW, offset) for offset in range(blocks_back, 0, -1)]
    joined = jnp.concatenate(earlier + [both], axis=0)
    all_keys = joined[:, :kv_local]
    all_values = joined[:, kv_local:]
    key_pos = (
        positions[0] - blocks_back * rows + jnp.arange((blocks_back + 1) * rows, dtype=jnp.int32)
    )
    grouped = query.reshape(rows, kv_local, group, HD)
    scores = jnp.einsum(
        "tkgd,skd->kgts", grouped, all_keys, preferred_element_type=jnp.float32
    ) * QUERY_SCALAR ** (-0.5)
    distance = positions[:, None] - key_pos[None, :]
    allowed = (distance >= 0) & (distance < WINDOW) & (key_pos[None, :] >= 0)
    expo = jnp.where(allowed, jnp.exp(scores), 0.0)
    total = jnp.sum(expo, axis=-1, keepdims=True)
    probs = (expo / total).astype(jnp.bfloat16)
    output = jnp.einsum("kgts,skd->tkgd", probs, all_values, preferred_element_type=jnp.float32)
    return output.reshape(rows, query_cols).astype(jnp.bfloat16)


CORES_PER_CHIP = 2
GAIN_ROWS = 8
TILE_ROWS = 16


def solution(mesh):
    rows, cols = mesh.shape["row"], mesh.shape["col"]
    minor = len({tuple(getattr(d, "coords", (0,)))[0] for d in mesh.devices[:, 0].flat})
    if rows % minor:
        minor = 1
    split = Mesh(
        mesh.devices.reshape(rows // minor, minor, cols // CORES_PER_CHIP, CORES_PER_CHIP),
        ("rz", "rx", "cy", "cc"),
    )
    col = ("cy", "cc")
    placed = (
        P(ROW, col),
        P(col),
        P(),
        P(),
        P(ROW, col),
        P(ROW, col),
        P(ROW, col),
    )
    return jax.shard_map(
        local, mesh=split, in_specs=placed, out_specs=P(ROW, col), check_vma=False
    )
```

```python
import jax
import jax.numpy as jnp
from jax import lax
from jax.sharding import Mesh, PartitionSpec as P

D = 5376
HD = 128
WINDOW = 1024


EPS = 1e-06
CLIP_FRACTION = 0.25
QUERY_SCALAR = 168.0
ROPE_BASE = 10000.0


ROW = ("rz", "rx")


def shifted(array, axis, by):
    peers = lax.axis_size(axis)
    pairs = [(i, i + by) for i in range(peers) if 0 <= i + by < peers]
    return lax.ppermute(array, axis, pairs)


def ring_gather(parts, axis, dims):
    peers = lax.axis_size(axis)
    right = [(i, (i + 1) % peers) for i in range(peers)]
    left = [(i, (i - 1) % peers) for i in range(peers)]
    held = {0: parts}
    forward = parts
    backward = parts
    for step in range(1, peers // 2 + 1):
        forward = lax.ppermute(forward, axis, right)
        held[peers - step] = forward
        if step < peers - step:
            backward = lax.ppermute(backward, axis, left)
            held[step] = backward
    start = (peers - lax.axis_index(axis)) % peers
    out = []
    for leaf, (dim) in enumerate(dims):
        stacked = jnp.concatenate([held[k][leaf] for k in range(peers)], axis=dim)
        doubled = jnp.concatenate([stacked, stacked], axis=dim)
        size = parts[leaf].shape[dim]
        out.append(lax.dynamic_slice_in_dim(doubled, start * size, peers * size, dim))
    return tuple(out)


def clip_with(weight, largest):
    bound = CLIP_FRACTION * largest
    return jnp.clip(weight.astype(jnp.float32), -bound, bound).astype(jnp.bfloat16)


def column_max(weight):
    return jnp.max(jnp.abs(weight.astype(jnp.float32)), axis=0)


def head_norm(values, head_gain):
    return values * lax.rsqrt(jnp.mean(values * values, axis=-1, keepdims=True) + EPS) * head_gain


def rotate(values, positions):
    half = values.shape[-1] // 2
    freqs = ROPE_BASE ** (-(jnp.arange(half, dtype=jnp.float32) * 2.0 / values.shape[-1]))
    angles = positions.astype(jnp.float32)[:, None] * freqs[None, :]
    cosine = jnp.cos(angles)[:, None, :]
    sine = jnp.sin(angles)[:, None, :]
    first = values[..., :half]
    second = values[..., half:]
    return jnp.concatenate(
        [first * cosine - second * sine, second * cosine + first * sine], axis=-1
    )


def local(tokens, gain, query_gain, key_gain, w_query, w_key, w_value):
    rows = tokens.shape[0]
    query_cols = w_query.shape[1]
    key_cols = w_key.shape[1]
    stacked = jnp.concatenate([w_query, w_key, w_value], axis=1)
    weight_rows, weight_cols = stacked.shape
    aligned = -(-(weight_rows + 1) // TILE_ROWS) * TILE_ROWS
    local_max = jnp.max(jnp.abs(stacked), axis=0)
    padded = jnp.concatenate(
        [
            stacked,
            local_max[None],
            jnp.zeros((aligned - weight_rows - 1, weight_cols), stacked.dtype),
        ],
        axis=0,
    )
    slabs = lax.all_gather(padded, ROW, axis=0, tiled=True).reshape(-1, aligned, weight_cols)
    largest = jnp.max(slabs[:, weight_rows].astype(jnp.float32), axis=0)
    clipped = clip_with(slabs.reshape(-1, weight_cols), largest)
    rows_tokens, piece = tokens.shape
    cores = lax.axis_size("cc")
    high = gain.astype(jnp.bfloat16)
    rest = gain - high.astype(jnp.float32)
    middle = rest.astype(jnp.bfloat16)
    low = (rest - middle.astype(jnp.float32)).astype(jnp.bfloat16)
    filler = jnp.zeros((GAIN_ROWS - 3, piece), jnp.bfloat16)
    packed = jnp.concatenate([tokens, high[None], middle[None], low[None], filler], axis=0)
    (along_y,) = ring_gather((packed,), "cy", (1,))
    (along_all,) = ring_gather((along_y,), "cc", (1,))
    blocks = along_all.shape[1] // (cores * piece)
    split = along_all[rows_tokens : rows_tokens + 3].astype(jnp.float32)
    full_gain = split[0] + (split[1] + split[2])
    widened = along_all[:rows_tokens].astype(jnp.float32)
    squares = jnp.sum(widened * widened, axis=1)
    inverse = lax.rsqrt(squares / D + EPS)[:, None]
    normed = (widened * inverse * full_gain[None, :]).astype(jnp.bfloat16)
    halves = piece // weight_rows
    whole = jnp.pad(
        normed.reshape(rows_tokens, cores, blocks, halves, weight_rows)
        .transpose(0, 2, 1, 3, 4)
        .reshape(rows_tokens, -1, weight_rows),
        ((0, 0), (0, 0), (0, aligned - weight_rows)),
    ).reshape(rows_tokens, -1)
    ordered = clipped
    kv_part = jnp.dot(whole, ordered[:, query_cols:], preferred_element_type=jnp.float32)
    keys = kv_part[:, :key_cols]
    values = kv_part[:, key_cols:]
    query = jnp.dot(whole, ordered[:, :query_cols], preferred_element_type=jnp.float32)
    heads_local = query_cols // HD
    kv_local = key_cols // HD
    group = heads_local // kv_local
    positions = lax.axis_index(ROW) * rows + jnp.arange(rows, dtype=jnp.int32)
    query = rotate(head_norm(query.reshape(rows, heads_local, HD), query_gain), positions).astype(
        jnp.bfloat16
    )
    keys = rotate(head_norm(keys.reshape(rows, kv_local, HD), key_gain), positions).astype(
        jnp.bfloat16
    )
    values = values.reshape(rows, kv_local, HD).astype(jnp.bfloat16)
    blocks_back = WINDOW // rows
    both = jnp.concatenate([keys, values], axis=1)
    earlier = [shifted(both, ROW, offset) for offset in range(blocks_back, 0, -1)]
    joined = jnp.concatenate(earlier + [both], axis=0)
    all_keys = joined[:, :kv_local]
    all_values = joined[:, kv_local:]
    key_pos = (
        positions[0] - blocks_back * rows + jnp.arange((blocks_back + 1) * rows, dtype=jnp.int32)
    )
    grouped = query.reshape(rows, kv_local, group, HD)
    scores = jnp.einsum(
        "tkgd,skd->kgts", grouped, all_keys, preferred_element_type=jnp.float32
    ) * QUERY_SCALAR ** (-0.5)
    distance = positions[:, None] - key_pos[None, :]
    allowed = (distance >= 0) & (distance < WINDOW) & (key_pos[None, :] >= 0)
    expo = jnp.where(allowed, jnp.exp(scores), 0.0)
    total = jnp.sum(expo, axis=-1, keepdims=True)
    probs = (expo / total).astype(jnp.bfloat16)
    output = jnp.einsum("kgts,skd->tkgd", probs, all_values, preferred_element_type=jnp.float32)
    return output.reshape(rows, query_cols).astype(jnp.bfloat16)


CORES_PER_CHIP = 2
GAIN_ROWS = 8
TILE_ROWS = 16


def solution(mesh):
    rows, cols = mesh.shape["row"], mesh.shape["col"]
    minor = len({tuple(getattr(d, "coords", (0,)))[0] for d in mesh.devices[:, 0].flat})
    if rows % minor:
        minor = 1
    split = Mesh(
        mesh.devices.reshape(rows // minor, minor, cols // CORES_PER_CHIP, CORES_PER_CHIP),
        ("rz", "rx", "cy", "cc"),
    )
    col = ("cy", "cc")
    placed = (
        P(ROW, col),
        P(col),
        P(),
        P(),
        P(ROW, col),
        P(ROW, col),
        P(ROW, col),
    )
    return jax.shard_map(
        local, mesh=split, in_specs=placed, out_specs=P(ROW, col), check_vma=False
    )
```

```python
import jax
import jax.numpy as jnp
from jax import lax
from jax.sharding import Mesh, PartitionSpec as P

D = 5376
HD = 128
WINDOW = 1024


EPS = 1e-06
CLIP_FRACTION = 0.25
QUERY_SCALAR = 168.0
ROPE_BASE = 10000.0


ROW = ("rz", "rx")


def shifted(array, axis, by):
    peers = lax.axis_size(axis)
    pairs = [(i, i + by) for i in range(peers) if 0 <= i + by < peers]
    return lax.ppermute(array, axis, pairs)


def ring_gather(parts, axis, dims):
    peers = lax.axis_size(axis)
    right = [(i, (i + 1) % peers) for i in range(peers)]
    left = [(i, (i - 1) % peers) for i in range(peers)]
    held = {0: parts}
    forward = parts
    backward = parts
    for step in range(1, peers // 2 + 1):
        forward = lax.ppermute(forward, axis, right)
        held[peers - step] = forward
        if step < peers - step:
            backward = lax.ppermute(backward, axis, left)
            held[step] = backward
    start = (peers - lax.axis_index(axis)) % peers
    out = []
    for leaf, (dim) in enumerate(dims):
        stacked = jnp.concatenate([held[k][leaf] for k in range(peers)], axis=dim)
        doubled = jnp.concatenate([stacked, stacked], axis=dim)
        size = parts[leaf].shape[dim]
        out.append(lax.dynamic_slice_in_dim(doubled, start * size, peers * size, dim))
    return tuple(out)


def clip_with(weight, largest):
    bound = CLIP_FRACTION * largest
    return jnp.clip(weight.astype(jnp.float32), -bound, bound).astype(jnp.bfloat16)


def column_max(weight):
    return jnp.max(jnp.abs(weight.astype(jnp.float32)), axis=0)


def head_norm(values, head_gain):
    return values * lax.rsqrt(jnp.mean(values * values, axis=-1, keepdims=True) + EPS) * head_gain


def rotate(values, positions):
    half = values.shape[-1] // 2
    freqs = ROPE_BASE ** (-(jnp.arange(half, dtype=jnp.float32) * 2.0 / values.shape[-1]))
    angles = positions.astype(jnp.float32)[:, None] * freqs[None, :]
    cosine = jnp.cos(angles)[:, None, :]
    sine = jnp.sin(angles)[:, None, :]
    first = values[..., :half]
    second = values[..., half:]
    return jnp.concatenate(
        [first * cosine - second * sine, second * cosine + first * sine], axis=-1
    )


def local(tokens, gain, query_gain, key_gain, w_query, w_key, w_value):
    rows = tokens.shape[0]
    query_cols = w_query.shape[1]
    key_cols = w_key.shape[1]
    stacked = jnp.concatenate([w_query, w_key, w_value], axis=1)
    weight_rows, weight_cols = stacked.shape
    aligned = -(-(weight_rows + 1) // TILE_ROWS) * TILE_ROWS
    local_max = jnp.max(jnp.abs(stacked), axis=0)
    padded = jnp.concatenate(
        [
            stacked,
            local_max[None],
            jnp.zeros((aligned - weight_rows - 1, weight_cols), stacked.dtype),
        ],
        axis=0,
    )
    (along_x,) = ring_gather((padded,), "rx", (0,))
    slabs = lax.all_gather(along_x, "rz", axis=0, tiled=True).reshape(-1, aligned, weight_cols)
    largest = jnp.max(slabs[:, weight_rows].astype(jnp.float32), axis=0)
    clipped = clip_with(slabs[:, :weight_rows].reshape(-1, weight_cols), largest)
    rows_tokens, piece = tokens.shape
    cores = lax.axis_size("cc")
    high = gain.astype(jnp.bfloat16)
    rest = gain - high.astype(jnp.float32)
    middle = rest.astype(jnp.bfloat16)
    low = (rest - middle.astype(jnp.float32)).astype(jnp.bfloat16)
    filler = jnp.zeros((GAIN_ROWS - 3, piece), jnp.bfloat16)
    packed = jnp.concatenate([tokens, high[None], middle[None], low[None], filler], axis=0)
    (along_y,) = ring_gather((packed,), "cy", (1,))
    (along_all,) = ring_gather((along_y,), "cc", (1,))
    blocks = along_all.shape[1] // (cores * piece)
    split = along_all[rows_tokens : rows_tokens + 3].astype(jnp.float32)
    full_gain = split[0] + (split[1] + split[2])
    widened = along_all[:rows_tokens].astype(jnp.float32)
    squares = jnp.sum(widened * widened, axis=1)
    inverse = lax.rsqrt(squares / D + EPS)[:, None]
    whole = (widened * inverse * full_gain[None, :]).astype(jnp.bfloat16)
    ordered = (
        clipped.reshape(blocks, cores, piece, clipped.shape[1])
        .transpose(1, 0, 2, 3)
        .reshape(clipped.shape)
    )
    kv_part = jnp.dot(whole, ordered[:, query_cols:], preferred_element_type=jnp.float32)
    keys = kv_part[:, :key_cols]
    values = kv_part[:, key_cols:]
    query = jnp.dot(whole, ordered[:, :query_cols], preferred_element_type=jnp.float32)
    heads_local = query_cols // HD
    kv_local = key_cols // HD
    group = heads_local // kv_local
    positions = lax.axis_index(ROW) * rows + jnp.arange(rows, dtype=jnp.int32)
    query = rotate(head_norm(query.reshape(rows, heads_local, HD), query_gain), positions).astype(
        jnp.bfloat16
    )
    keys = rotate(head_norm(keys.reshape(rows, kv_local, HD), key_gain), positions).astype(
        jnp.bfloat16
    )
    values = values.reshape(rows, kv_local, HD).astype(jnp.bfloat16)
    blocks_back = WINDOW // rows
    both = jnp.concatenate([keys, values], axis=1)
    earlier = [shifted(both, ROW, offset) for offset in range(blocks_back, 0, -1)]
    joined = jnp.concatenate(earlier + [both], axis=0)
    all_keys = joined[:, :kv_local]
    all_values = joined[:, kv_local:]
    key_pos = (
        positions[0] - blocks_back * rows + jnp.arange((blocks_back + 1) * rows, dtype=jnp.int32)
    )
    grouped = query.reshape(rows, kv_local, group, HD)
    scores = jnp.einsum(
        "tkgd,skd->kgts", grouped, all_keys, preferred_element_type=jnp.float32
    ) * QUERY_SCALAR ** (-0.5)
    distance = positions[:, None] - key_pos[None, :]
    allowed = (distance >= 0) & (distance < WINDOW) & (key_pos[None, :] >= 0)
    expo = jnp.where(allowed, jnp.exp(scores), 0.0)
    total = jnp.sum(expo, axis=-1, keepdims=True)
    probs = (expo / total).astype(jnp.bfloat16)
    output = jnp.einsum("kgts,skd->tkgd", probs, all_values, preferred_element_type=jnp.float32)
    return output.reshape(rows, query_cols).astype(jnp.bfloat16)


CORES_PER_CHIP = 2
GAIN_ROWS = 8
TILE_ROWS = 16


def solution(mesh):
    rows, cols = mesh.shape["row"], mesh.shape["col"]
    minor = len({tuple(getattr(d, "coords", (0,)))[0] for d in mesh.devices[:, 0].flat})
    if rows % minor:
        minor = 1
    split = Mesh(
        mesh.devices.reshape(rows // minor, minor, cols // CORES_PER_CHIP, CORES_PER_CHIP),
        ("rz", "rx", "cy", "cc"),
    )
    col = ("cy", "cc")
    placed = (
        P(ROW, col),
        P(col),
        P(),
        P(),
        P(ROW, col),
        P(ROW, col),
        P(ROW, col),
    )
    return jax.shard_map(
        local, mesh=split, in_specs=placed, out_specs=P(ROW, col), check_vma=False
    )
```

```python
import jax
import jax.numpy as jnp
from jax import lax
from jax.sharding import Mesh, PartitionSpec as P

D = 5376
HD = 128
WINDOW = 1024


EPS = 1e-06
CLIP_FRACTION = 0.25
QUERY_SCALAR = 168.0
ROPE_BASE = 10000.0


ROW = ("rz", "rx")


def shifted(array, axis, by):
    peers = lax.axis_size(axis)
    pairs = [(i, i + by) for i in range(peers) if 0 <= i + by < peers]
    return lax.ppermute(array, axis, pairs)


def ring_gather(parts, axis, dims):
    peers = lax.axis_size(axis)
    right = [(i, (i + 1) % peers) for i in range(peers)]
    left = [(i, (i - 1) % peers) for i in range(peers)]
    held = {0: parts}
    forward = parts
    backward = parts
    for step in range(1, peers // 2 + 1):
        forward = lax.ppermute(forward, axis, right)
        held[peers - step] = forward
        if step < peers - step:
            backward = lax.ppermute(backward, axis, left)
            held[step] = backward
    start = (peers - lax.axis_index(axis)) % peers
    out = []
    for leaf, (dim) in enumerate(dims):
        stacked = jnp.concatenate([held[k][leaf] for k in range(peers)], axis=dim)
        doubled = jnp.concatenate([stacked, stacked], axis=dim)
        size = parts[leaf].shape[dim]
        out.append(lax.dynamic_slice_in_dim(doubled, start * size, peers * size, dim))
    return tuple(out)


def clip_with(weight, largest):
    bound = CLIP_FRACTION * largest
    return jnp.clip(weight.astype(jnp.float32), -bound, bound).astype(jnp.bfloat16)


def column_max(weight):
    return jnp.max(jnp.abs(weight.astype(jnp.float32)), axis=0)


def head_norm(values, head_gain):
    return values * lax.rsqrt(jnp.mean(values * values, axis=-1, keepdims=True) + EPS) * head_gain


def rotate(values, positions):
    half = values.shape[-1] // 2
    freqs = ROPE_BASE ** (-(jnp.arange(half, dtype=jnp.float32) * 2.0 / values.shape[-1]))
    angles = positions.astype(jnp.float32)[:, None] * freqs[None, :]
    cosine = jnp.cos(angles)[:, None, :]
    sine = jnp.sin(angles)[:, None, :]
    first = values[..., :half]
    second = values[..., half:]
    return jnp.concatenate(
        [first * cosine - second * sine, second * cosine + first * sine], axis=-1
    )


def local(tokens, gain, query_gain, key_gain, w_query, w_key, w_value):
    rows = tokens.shape[0]
    query_cols = w_query.shape[1]
    key_cols = w_key.shape[1]
    stacked = jnp.concatenate([w_query, w_key, w_value], axis=1)
    weight_rows, weight_cols = stacked.shape
    aligned = -(-(weight_rows + 1) // TILE_ROWS) * TILE_ROWS
    local_max = jnp.max(jnp.abs(stacked), axis=0)
    padded = jnp.concatenate(
        [
            stacked,
            local_max[None],
            jnp.zeros((aligned - weight_rows - 1, weight_cols), stacked.dtype),
        ],
        axis=0,
    )
    slabs = lax.all_gather(padded, ROW, axis=0, tiled=True).reshape(-1, aligned, weight_cols)
    largest = jnp.max(slabs[:, weight_rows].astype(jnp.float32), axis=0)

    def clipped_columns(first, last):
        part = slabs[:, :weight_rows, first:last].reshape(-1, last - first)
        return clip_with(part, largest[first:last])

    rows_tokens, piece = tokens.shape
    cores = lax.axis_size("cc")
    high = gain.astype(jnp.bfloat16)
    rest = gain - high.astype(jnp.float32)
    middle = rest.astype(jnp.bfloat16)
    low = (rest - middle.astype(jnp.float32)).astype(jnp.bfloat16)
    filler = jnp.zeros((GAIN_ROWS - 3, piece), jnp.bfloat16)
    packed = jnp.concatenate([tokens, high[None], middle[None], low[None], filler], axis=0)
    (along_y,) = ring_gather((packed,), "cy", (1,))
    (along_all,) = ring_gather((along_y,), "cc", (1,))
    blocks = along_all.shape[1] // (cores * piece)
    split = along_all[rows_tokens : rows_tokens + 3].astype(jnp.float32)
    full_gain = split[0] + (split[1] + split[2])
    widened = along_all[:rows_tokens].astype(jnp.float32)
    squares = jnp.sum(widened * widened, axis=1)
    inverse = lax.rsqrt(squares / D + EPS)[:, None]
    whole = (widened * inverse * full_gain[None, :]).astype(jnp.bfloat16)
    def ordered(first, last):
        part = clipped_columns(first, last)
        return (
            part.reshape(blocks, cores, piece, last - first)
            .transpose(1, 0, 2, 3)
            .reshape(part.shape)
        )

    kv_part = jnp.dot(
        whole, ordered(query_cols, weight_cols), preferred_element_type=jnp.float32
    )
    keys = kv_part[:, :key_cols]
    values = kv_part[:, key_cols:]
    query = jnp.dot(whole, ordered(0, query_cols), preferred_element_type=jnp.float32)
    heads_local = query_cols // HD
    kv_local = key_cols // HD
    group = heads_local // kv_local
    positions = lax.axis_index(ROW) * rows + jnp.arange(rows, dtype=jnp.int32)
    query = rotate(head_norm(query.reshape(rows, heads_local, HD), query_gain), positions).astype(
        jnp.bfloat16
    )
    keys = rotate(head_norm(keys.reshape(rows, kv_local, HD), key_gain), positions).astype(
        jnp.bfloat16
    )
    values = values.reshape(rows, kv_local, HD).astype(jnp.bfloat16)
    blocks_back = WINDOW // rows
    both = jnp.concatenate([keys, values], axis=1)
    earlier = [shifted(both, ROW, offset) for offset in range(blocks_back, 0, -1)]
    joined = jnp.concatenate(earlier + [both], axis=0)
    all_keys = joined[:, :kv_local]
    all_values = joined[:, kv_local:]
    key_pos = (
        positions[0] - blocks_back * rows + jnp.arange((blocks_back + 1) * rows, dtype=jnp.int32)
    )
    grouped = query.reshape(rows, kv_local, group, HD)
    scores = jnp.einsum(
        "tkgd,skd->kgts", grouped, all_keys, preferred_element_type=jnp.float32
    ) * QUERY_SCALAR ** (-0.5)
    distance = positions[:, None] - key_pos[None, :]
    allowed = (distance >= 0) & (distance < WINDOW) & (key_pos[None, :] >= 0)
    expo = jnp.where(allowed, jnp.exp(scores), 0.0)
    total = jnp.sum(expo, axis=-1, keepdims=True)
    probs = (expo / total).astype(jnp.bfloat16)
    output = jnp.einsum("kgts,skd->tkgd", probs, all_values, preferred_element_type=jnp.float32)
    return output.reshape(rows, query_cols).astype(jnp.bfloat16)


CORES_PER_CHIP = 2
GAIN_ROWS = 8
TILE_ROWS = 16


def solution(mesh):
    rows, cols = mesh.shape["row"], mesh.shape["col"]
    minor = len({tuple(getattr(d, "coords", (0,)))[0] for d in mesh.devices[:, 0].flat})
    if rows % minor:
        minor = 1
    split = Mesh(
        mesh.devices.reshape(rows // minor, minor, cols // CORES_PER_CHIP, CORES_PER_CHIP),
        ("rz", "rx", "cy", "cc"),
    )
    col = ("cy", "cc")
    placed = (
        P(ROW, col),
        P(col),
        P(),
        P(),
        P(ROW, col),
        P(ROW, col),
        P(ROW, col),
    )
    return jax.shard_map(
        local, mesh=split, in_specs=placed, out_specs=P(ROW, col), check_vma=False
    )
```

```python
import jax
import jax.numpy as jnp
from jax import lax
from jax.sharding import Mesh, PartitionSpec as P

D = 5376
HD = 128
WINDOW = 1024


EPS = 1e-06
CLIP_FRACTION = 0.25
QUERY_SCALAR = 168.0
ROPE_BASE = 10000.0


ROW = ("rz", "rxh", "rxl")


def shifted(array, axis, by):
    peers = lax.axis_size(axis)
    pairs = [(i, i + by) for i in range(peers) if 0 <= i + by < peers]
    return lax.ppermute(array, axis, pairs)


def ring_gather(parts, axis, dims):
    peers = lax.axis_size(axis)
    right = [(i, (i + 1) % peers) for i in range(peers)]
    left = [(i, (i - 1) % peers) for i in range(peers)]
    held = {0: parts}
    forward = parts
    backward = parts
    for step in range(1, peers // 2 + 1):
        forward = lax.ppermute(forward, axis, right)
        held[peers - step] = forward
        if step < peers - step:
            backward = lax.ppermute(backward, axis, left)
            held[step] = backward
    start = (peers - lax.axis_index(axis)) % peers
    out = []
    for leaf, (dim) in enumerate(dims):
        stacked = jnp.concatenate([held[k][leaf] for k in range(peers)], axis=dim)
        doubled = jnp.concatenate([stacked, stacked], axis=dim)
        size = parts[leaf].shape[dim]
        out.append(lax.dynamic_slice_in_dim(doubled, start * size, peers * size, dim))
    return tuple(out)


def clip_with(weight, largest):
    bound = CLIP_FRACTION * largest
    return jnp.clip(weight.astype(jnp.float32), -bound, bound).astype(jnp.bfloat16)


def column_max(weight):
    return jnp.max(jnp.abs(weight.astype(jnp.float32)), axis=0)


def head_norm(values, head_gain):
    return values * lax.rsqrt(jnp.mean(values * values, axis=-1, keepdims=True) + EPS) * head_gain


def rotate(values, positions):
    half = values.shape[-1] // 2
    freqs = ROPE_BASE ** (-(jnp.arange(half, dtype=jnp.float32) * 2.0 / values.shape[-1]))
    angles = positions.astype(jnp.float32)[:, None] * freqs[None, :]
    cosine = jnp.cos(angles)[:, None, :]
    sine = jnp.sin(angles)[:, None, :]
    first = values[..., :half]
    second = values[..., half:]
    return jnp.concatenate(
        [first * cosine - second * sine, second * cosine + first * sine], axis=-1
    )


def local(tokens, gain, query_gain, key_gain, w_query, w_key, w_value):
    rows = tokens.shape[0]
    query_cols = w_query.shape[1]
    key_cols = w_key.shape[1]
    stacked = jnp.concatenate([w_query, w_key, w_value], axis=1)
    weight_rows, weight_cols = stacked.shape
    aligned = -(-(weight_rows + 1) // TILE_ROWS) * TILE_ROWS
    local_max = jnp.max(jnp.abs(stacked), axis=0)
    padded = jnp.concatenate(
        [
            stacked,
            local_max[None],
            jnp.zeros((aligned - weight_rows - 1, weight_cols), stacked.dtype),
        ],
        axis=0,
    )
    (paired,) = ring_gather((padded,), "rxl", (0,))
    slabs = lax.all_gather(paired, ("rz", "rxh"), axis=0, tiled=True).reshape(-1, aligned, weight_cols)
    largest = jnp.max(slabs[:, weight_rows].astype(jnp.float32), axis=0)

    def clipped_columns(first, last):
        part = slabs[:, :weight_rows, first:last].reshape(-1, last - first)
        return clip_with(part, largest[first:last])

    rows_tokens, piece = tokens.shape
    cores = lax.axis_size("cc")
    high = gain.astype(jnp.bfloat16)
    rest = gain - high.astype(jnp.float32)
    middle = rest.astype(jnp.bfloat16)
    low = (rest - middle.astype(jnp.float32)).astype(jnp.bfloat16)
    filler = jnp.zeros((GAIN_ROWS - 3, piece), jnp.bfloat16)
    packed = jnp.concatenate([tokens, high[None], middle[None], low[None], filler], axis=0)
    (along_y,) = ring_gather((packed,), "cy", (1,))
    (along_all,) = ring_gather((along_y,), "cc", (1,))
    blocks = along_all.shape[1] // (cores * piece)
    split = along_all[rows_tokens : rows_tokens + 3].astype(jnp.float32)
    full_gain = split[0] + (split[1] + split[2])
    widened = along_all[:rows_tokens].astype(jnp.float32)
    squares = jnp.sum(widened * widened, axis=1)
    inverse = lax.rsqrt(squares / D + EPS)[:, None]
    whole = (widened * inverse * full_gain[None, :]).astype(jnp.bfloat16)
    def ordered(first, last):
        part = clipped_columns(first, last)
        return (
            part.reshape(blocks, cores, piece, last - first)
            .transpose(1, 0, 2, 3)
            .reshape(part.shape)
        )

    kv_part = jnp.dot(
        whole, ordered(query_cols, weight_cols), preferred_element_type=jnp.float32
    )
    keys = kv_part[:, :key_cols]
    values = kv_part[:, key_cols:]
    query = jnp.dot(whole, ordered(0, query_cols), preferred_element_type=jnp.float32)
    heads_local = query_cols // HD
    kv_local = key_cols // HD
    group = heads_local // kv_local
    positions = lax.axis_index(ROW) * rows + jnp.arange(rows, dtype=jnp.int32)
    query = rotate(head_norm(query.reshape(rows, heads_local, HD), query_gain), positions).astype(
        jnp.bfloat16
    )
    keys = rotate(head_norm(keys.reshape(rows, kv_local, HD), key_gain), positions).astype(
        jnp.bfloat16
    )
    values = values.reshape(rows, kv_local, HD).astype(jnp.bfloat16)
    blocks_back = WINDOW // rows
    both = jnp.concatenate([keys, values], axis=1)
    earlier = [shifted(both, ROW, offset) for offset in range(blocks_back, 0, -1)]
    joined = jnp.concatenate(earlier + [both], axis=0)
    all_keys = joined[:, :kv_local]
    all_values = joined[:, kv_local:]
    key_pos = (
        positions[0] - blocks_back * rows + jnp.arange((blocks_back + 1) * rows, dtype=jnp.int32)
    )
    grouped = query.reshape(rows, kv_local, group, HD)
    scores = jnp.einsum(
        "tkgd,skd->kgts", grouped, all_keys, preferred_element_type=jnp.float32
    ) * QUERY_SCALAR ** (-0.5)
    distance = positions[:, None] - key_pos[None, :]
    allowed = (distance >= 0) & (distance < WINDOW) & (key_pos[None, :] >= 0)
    expo = jnp.where(allowed, jnp.exp(scores), 0.0)
    total = jnp.sum(expo, axis=-1, keepdims=True)
    probs = (expo / total).astype(jnp.bfloat16)
    output = jnp.einsum("kgts,skd->tkgd", probs, all_values, preferred_element_type=jnp.float32)
    return output.reshape(rows, query_cols).astype(jnp.bfloat16)


CORES_PER_CHIP = 2
GAIN_ROWS = 8
TILE_ROWS = 16


def solution(mesh):
    rows, cols = mesh.shape["row"], mesh.shape["col"]
    minor = len({tuple(getattr(d, "coords", (0,)))[0] for d in mesh.devices[:, 0].flat})
    if rows % minor:
        minor = 1
    pair = 2 if minor % 2 == 0 else 1
    split = Mesh(
        mesh.devices.reshape(
            rows // minor, minor // pair, pair, cols // CORES_PER_CHIP, CORES_PER_CHIP
        ),
        ("rz", "rxh", "rxl", "cy", "cc"),
    )
    col = ("cy", "cc")
    placed = (
        P(ROW, col),
        P(col),
        P(),
        P(),
        P(ROW, col),
        P(ROW, col),
        P(ROW, col),
    )
    return jax.shard_map(
        local, mesh=split, in_specs=placed, out_specs=P(ROW, col), check_vma=False
    )
```

```python
import jax
import jax.numpy as jnp
from jax import lax
from jax.experimental import pallas as pl
from jax.sharding import Mesh, PartitionSpec as P

D = 5376
HD = 128
WINDOW = 1024


EPS = 1e-06
CLIP_FRACTION = 0.25
QUERY_SCALAR = 168.0
ROPE_BASE = 10000.0


ROW = ("rz", "rx")


def shifted(array, axis, by):
    peers = lax.axis_size(axis)
    pairs = [(i, i + by) for i in range(peers) if 0 <= i + by < peers]
    return lax.ppermute(array, axis, pairs)


def ring_gather(parts, axis, dims):
    peers = lax.axis_size(axis)
    right = [(i, (i + 1) % peers) for i in range(peers)]
    left = [(i, (i - 1) % peers) for i in range(peers)]
    held = {0: parts}
    forward = parts
    backward = parts
    for step in range(1, peers // 2 + 1):
        forward = lax.ppermute(forward, axis, right)
        held[peers - step] = forward
        if step < peers - step:
            backward = lax.ppermute(backward, axis, left)
            held[step] = backward
    start = (peers - lax.axis_index(axis)) % peers
    out = []
    for leaf, (dim) in enumerate(dims):
        stacked = jnp.concatenate([held[k][leaf] for k in range(peers)], axis=dim)
        doubled = jnp.concatenate([stacked, stacked], axis=dim)
        size = parts[leaf].shape[dim]
        out.append(lax.dynamic_slice_in_dim(doubled, start * size, peers * size, dim))
    return tuple(out)


def project_kernel(bound_ref, token_ref, slab_ref, out_ref):
    @pl.when(pl.program_id(0) == 0)
    def _():
        out_ref[...] = jnp.zeros_like(out_ref)

    bound = bound_ref[...]
    total = out_ref[...]
    for i in range(token_ref.shape[0]):
        weight = slab_ref[i].astype(jnp.float32)
        clipped = jnp.clip(weight, -bound, bound).astype(jnp.bfloat16)
        total = total + jnp.dot(token_ref[i], clipped, preferred_element_type=jnp.float32)
    out_ref[...] = total


def project(bound, token_slabs, slabs):
    count, rows, depth = token_slabs.shape
    cols = slabs.shape[2]
    group = SLABS_PER_STEP
    return pl.pallas_call(
        project_kernel,
        grid=(count // group,),
        in_specs=[
            pl.BlockSpec((1, cols), lambda g: (0, 0)),
            pl.BlockSpec((group, rows, depth), lambda g: (g, 0, 0)),
            pl.BlockSpec((group, depth, cols), lambda g: (g, 0, 0)),
        ],
        out_specs=pl.BlockSpec((rows, cols), lambda g: (0, 0)),
        out_shape=jax.ShapeDtypeStruct((rows, cols), jnp.float32),
    )(bound, token_slabs, slabs)


def clip_with(weight, largest):
    bound = CLIP_FRACTION * largest
    return jnp.clip(weight.astype(jnp.float32), -bound, bound).astype(jnp.bfloat16)


def column_max(weight):
    return jnp.max(jnp.abs(weight.astype(jnp.float32)), axis=0)


def head_norm(values, head_gain):
    return values * lax.rsqrt(jnp.mean(values * values, axis=-1, keepdims=True) + EPS) * head_gain


def rotate(values, positions):
    half = values.shape[-1] // 2
    freqs = ROPE_BASE ** (-(jnp.arange(half, dtype=jnp.float32) * 2.0 / values.shape[-1]))
    angles = positions.astype(jnp.float32)[:, None] * freqs[None, :]
    cosine = jnp.cos(angles)[:, None, :]
    sine = jnp.sin(angles)[:, None, :]
    first = values[..., :half]
    second = values[..., half:]
    return jnp.concatenate(
        [first * cosine - second * sine, second * cosine + first * sine], axis=-1
    )


def local(tokens, gain, query_gain, key_gain, w_query, w_key, w_value):
    rows = tokens.shape[0]
    query_cols = w_query.shape[1]
    key_cols = w_key.shape[1]
    stacked = jnp.concatenate([w_query, w_key, w_value], axis=1)
    weight_rows, weight_cols = stacked.shape
    aligned = -(-(weight_rows + 1) // TILE_ROWS) * TILE_ROWS
    local_max = jnp.max(jnp.abs(stacked), axis=0)
    padded = jnp.concatenate(
        [
            stacked,
            local_max[None],
            jnp.zeros((aligned - weight_rows - 1, weight_cols), stacked.dtype),
        ],
        axis=0,
    )
    slabs = lax.all_gather(padded, ROW, axis=0, tiled=True).reshape(-1, aligned, weight_cols)
    largest = jnp.max(slabs[:, weight_rows].astype(jnp.float32), axis=0)

    rows_tokens, piece = tokens.shape
    cores = lax.axis_size("cc")
    high = gain.astype(jnp.bfloat16)
    rest = gain - high.astype(jnp.float32)
    middle = rest.astype(jnp.bfloat16)
    low = (rest - middle.astype(jnp.float32)).astype(jnp.bfloat16)
    filler = jnp.zeros((GAIN_ROWS - 3, piece), jnp.bfloat16)
    packed = jnp.concatenate([tokens, high[None], middle[None], low[None], filler], axis=0)
    (along_y,) = ring_gather((packed,), "cy", (1,))
    (along_all,) = ring_gather((along_y,), "cc", (1,))
    blocks = along_all.shape[1] // (cores * piece)
    split = along_all[rows_tokens : rows_tokens + 3].astype(jnp.float32)
    full_gain = split[0] + (split[1] + split[2])
    widened = along_all[:rows_tokens].astype(jnp.float32)
    squares = jnp.sum(widened * widened, axis=1)
    inverse = lax.rsqrt(squares / D + EPS)[:, None]
    normed = (widened * inverse * full_gain[None, :]).astype(jnp.bfloat16)
    halves = piece // weight_rows
    token_slabs = jnp.pad(
        normed.reshape(rows_tokens, cores, blocks, halves, weight_rows)
        .transpose(2, 1, 3, 0, 4)
        .reshape(-1, rows_tokens, weight_rows),
        ((0, 0), (0, 0), (0, aligned - weight_rows)),
    )
    bound = (CLIP_FRACTION * largest)[None, :]
    projected = project(bound, token_slabs, slabs)
    query = projected[:, :query_cols]
    keys = projected[:, query_cols : query_cols + key_cols]
    values = projected[:, query_cols + key_cols :]
    heads_local = query_cols // HD
    kv_local = key_cols // HD
    group = heads_local // kv_local
    positions = lax.axis_index(ROW) * rows + jnp.arange(rows, dtype=jnp.int32)
    query = rotate(head_norm(query.reshape(rows, heads_local, HD), query_gain), positions).astype(
        jnp.bfloat16
    )
    keys = rotate(head_norm(keys.reshape(rows, kv_local, HD), key_gain), positions).astype(
        jnp.bfloat16
    )
    values = values.reshape(rows, kv_local, HD).astype(jnp.bfloat16)
    blocks_back = WINDOW // rows
    both = jnp.concatenate([keys, values], axis=1)
    earlier = [shifted(both, ROW, offset) for offset in range(blocks_back, 0, -1)]
    joined = jnp.concatenate(earlier + [both], axis=0)
    all_keys = joined[:, :kv_local]
    all_values = joined[:, kv_local:]
    key_pos = (
        positions[0] - blocks_back * rows + jnp.arange((blocks_back + 1) * rows, dtype=jnp.int32)
    )
    grouped = query.reshape(rows, kv_local, group, HD)
    scores = jnp.einsum(
        "tkgd,skd->kgts", grouped, all_keys, preferred_element_type=jnp.float32
    ) * QUERY_SCALAR ** (-0.5)
    distance = positions[:, None] - key_pos[None, :]
    allowed = (distance >= 0) & (distance < WINDOW) & (key_pos[None, :] >= 0)
    expo = jnp.where(allowed, jnp.exp(scores), 0.0)
    total = jnp.sum(expo, axis=-1, keepdims=True)
    probs = (expo / total).astype(jnp.bfloat16)
    output = jnp.einsum("kgts,skd->tkgd", probs, all_values, preferred_element_type=jnp.float32)
    return output.reshape(rows, query_cols).astype(jnp.bfloat16)


CORES_PER_CHIP = 2
GAIN_ROWS = 8
TILE_ROWS = 16
SLABS_PER_STEP = 4


def solution(mesh):
    rows, cols = mesh.shape["row"], mesh.shape["col"]
    minor = len({tuple(getattr(d, "coords", (0,)))[0] for d in mesh.devices[:, 0].flat})
    if rows % minor:
        minor = 1
    split = Mesh(
        mesh.devices.reshape(rows // minor, minor, cols // CORES_PER_CHIP, CORES_PER_CHIP),
        ("rz", "rx", "cy", "cc"),
    )
    col = ("cy", "cc")
    placed = (
        P(ROW, col),
        P(col),
        P(),
        P(),
        P(ROW, col),
        P(ROW, col),
        P(ROW, col),
    )
    return jax.shard_map(
        local, mesh=split, in_specs=placed, out_specs=P(ROW, col), check_vma=False
    )
```

```python
import jax
import jax.numpy as jnp
from jax import lax
from jax.sharding import Mesh, PartitionSpec as P

D = 5376
HD = 128
WINDOW = 1024


EPS = 1e-06
CLIP_FRACTION = 0.25
QUERY_SCALAR = 168.0
ROPE_BASE = 10000.0


ROW = ("rz", "rx")


def shifted(array, axis, by):
    peers = lax.axis_size(axis)
    pairs = [(i, i + by) for i in range(peers) if 0 <= i + by < peers]
    return lax.ppermute(array, axis, pairs)


def ring_gather(parts, axis, dims):
    peers = lax.axis_size(axis)
    right = [(i, (i + 1) % peers) for i in range(peers)]
    left = [(i, (i - 1) % peers) for i in range(peers)]
    held = {0: parts}
    forward = parts
    backward = parts
    for step in range(1, peers // 2 + 1):
        forward = lax.ppermute(forward, axis, right)
        held[peers - step] = forward
        if step < peers - step:
            backward = lax.ppermute(backward, axis, left)
            held[step] = backward
    start = (peers - lax.axis_index(axis)) % peers
    out = []
    for leaf, (dim) in enumerate(dims):
        stacked = jnp.concatenate([held[k][leaf] for k in range(peers)], axis=dim)
        doubled = jnp.concatenate([stacked, stacked], axis=dim)
        size = parts[leaf].shape[dim]
        out.append(lax.dynamic_slice_in_dim(doubled, start * size, peers * size, dim))
    return tuple(out)


def clip_with(weight, largest):
    bound = CLIP_FRACTION * largest
    return jnp.clip(weight.astype(jnp.float32), -bound, bound).astype(jnp.bfloat16)


def column_max(weight):
    return jnp.max(jnp.abs(weight.astype(jnp.float32)), axis=0)


def head_norm(values, head_gain):
    return values * lax.rsqrt(jnp.mean(values * values, axis=-1, keepdims=True) + EPS) * head_gain


def rotate(values, positions):
    half = values.shape[-1] // 2
    freqs = ROPE_BASE ** (-(jnp.arange(half, dtype=jnp.float32) * 2.0 / values.shape[-1]))
    angles = positions.astype(jnp.float32)[:, None] * freqs[None, :]
    cosine = jnp.cos(angles)[:, None, :]
    sine = jnp.sin(angles)[:, None, :]
    first = values[..., :half]
    second = values[..., half:]
    return jnp.concatenate(
        [first * cosine - second * sine, second * cosine + first * sine], axis=-1
    )


def local(tokens, gain, query_gain, key_gain, w_query, w_key, w_value):
    rows = tokens.shape[0]
    query_cols = w_query.shape[1]
    key_cols = w_key.shape[1]
    stacked = jnp.concatenate([w_query, w_key, w_value], axis=1)
    weight_rows, weight_cols = stacked.shape
    aligned = -(-(weight_rows + 1) // TILE_ROWS) * TILE_ROWS
    local_max = jnp.max(jnp.abs(stacked), axis=0)
    padded = jnp.concatenate(
        [
            stacked,
            local_max[None],
            jnp.zeros((aligned - weight_rows - 1, weight_cols), stacked.dtype),
        ],
        axis=0,
    )
    placed = jnp.zeros((lax.axis_size(ROW), aligned, weight_cols), padded.dtype)
    placed = lax.dynamic_update_slice_in_dim(placed, padded[None], lax.axis_index(ROW), 0)
    slabs = lax.psum(placed, ROW)
    largest = jnp.max(slabs[:, weight_rows].astype(jnp.float32), axis=0)

    def clipped_columns(first, last):
        part = slabs[:, :weight_rows, first:last].reshape(-1, last - first)
        return clip_with(part, largest[first:last])

    rows_tokens, piece = tokens.shape
    cores = lax.axis_size("cc")
    high = gain.astype(jnp.bfloat16)
    rest = gain - high.astype(jnp.float32)
    middle = rest.astype(jnp.bfloat16)
    low = (rest - middle.astype(jnp.float32)).astype(jnp.bfloat16)
    filler = jnp.zeros((GAIN_ROWS - 3, piece), jnp.bfloat16)
    packed = jnp.concatenate([tokens, high[None], middle[None], low[None], filler], axis=0)
    (along_y,) = ring_gather((packed,), "cy", (1,))
    (along_all,) = ring_gather((along_y,), "cc", (1,))
    blocks = along_all.shape[1] // (cores * piece)
    split = along_all[rows_tokens : rows_tokens + 3].astype(jnp.float32)
    full_gain = split[0] + (split[1] + split[2])
    widened = along_all[:rows_tokens].astype(jnp.float32)
    squares = jnp.sum(widened * widened, axis=1)
    inverse = lax.rsqrt(squares / D + EPS)[:, None]
    whole = (widened * inverse * full_gain[None, :]).astype(jnp.bfloat16)
    def ordered(first, last):
        part = clipped_columns(first, last)
        return (
            part.reshape(blocks, cores, piece, last - first)
            .transpose(1, 0, 2, 3)
            .reshape(part.shape)
        )

    kv_part = jnp.dot(
        whole, ordered(query_cols, weight_cols), preferred_element_type=jnp.float32
    )
    keys = kv_part[:, :key_cols]
    values = kv_part[:, key_cols:]
    query = jnp.dot(whole, ordered(0, query_cols), preferred_element_type=jnp.float32)
    heads_local = query_cols // HD
    kv_local = key_cols // HD
    group = heads_local // kv_local
    positions = lax.axis_index(ROW) * rows + jnp.arange(rows, dtype=jnp.int32)
    query = rotate(head_norm(query.reshape(rows, heads_local, HD), query_gain), positions).astype(
        jnp.bfloat16
    )
    keys = rotate(head_norm(keys.reshape(rows, kv_local, HD), key_gain), positions).astype(
        jnp.bfloat16
    )
    values = values.reshape(rows, kv_local, HD).astype(jnp.bfloat16)
    blocks_back = WINDOW // rows
    both = jnp.concatenate([keys, values], axis=1)
    earlier = [shifted(both, ROW, offset) for offset in range(blocks_back, 0, -1)]
    joined = jnp.concatenate(earlier + [both], axis=0)
    all_keys = joined[:, :kv_local]
    all_values = joined[:, kv_local:]
    key_pos = (
        positions[0] - blocks_back * rows + jnp.arange((blocks_back + 1) * rows, dtype=jnp.int32)
    )
    grouped = query.reshape(rows, kv_local, group, HD)
    scores = jnp.einsum(
        "tkgd,skd->kgts", grouped, all_keys, preferred_element_type=jnp.float32
    ) * QUERY_SCALAR ** (-0.5)
    distance = positions[:, None] - key_pos[None, :]
    allowed = (distance >= 0) & (distance < WINDOW) & (key_pos[None, :] >= 0)
    expo = jnp.where(allowed, jnp.exp(scores), 0.0)
    total = jnp.sum(expo, axis=-1, keepdims=True)
    probs = (expo / total).astype(jnp.bfloat16)
    output = jnp.einsum("kgts,skd->tkgd", probs, all_values, preferred_element_type=jnp.float32)
    return output.reshape(rows, query_cols).astype(jnp.bfloat16)


CORES_PER_CHIP = 2
GAIN_ROWS = 8
TILE_ROWS = 16


def solution(mesh):
    rows, cols = mesh.shape["row"], mesh.shape["col"]
    minor = len({tuple(getattr(d, "coords", (0,)))[0] for d in mesh.devices[:, 0].flat})
    if rows % minor:
        minor = 1
    split = Mesh(
        mesh.devices.reshape(rows // minor, minor, cols // CORES_PER_CHIP, CORES_PER_CHIP),
        ("rz", "rx", "cy", "cc"),
    )
    col = ("cy", "cc")
    placed = (
        P(ROW, col),
        P(col),
        P(),
        P(),
        P(ROW, col),
        P(ROW, col),
        P(ROW, col),
    )
    return jax.shard_map(
        local, mesh=split, in_specs=placed, out_specs=P(ROW, col), check_vma=False
    )
```

```python
import jax
import jax.numpy as jnp
from jax import lax
from jax.sharding import Mesh, PartitionSpec as P

D = 5376
HD = 128
WINDOW = 1024


EPS = 1e-06
CLIP_FRACTION = 0.25
QUERY_SCALAR = 168.0
ROPE_BASE = 10000.0


ROW = ("rz", "rx")


def shifted(array, axis, by):
    peers = lax.axis_size(axis)
    pairs = [(i, i + by) for i in range(peers) if 0 <= i + by < peers]
    return lax.ppermute(array, axis, pairs)


def ring_gather(parts, axis, dims):
    peers = lax.axis_size(axis)
    right = [(i, (i + 1) % peers) for i in range(peers)]
    left = [(i, (i - 1) % peers) for i in range(peers)]
    held = {0: parts}
    forward = parts
    backward = parts
    for step in range(1, peers // 2 + 1):
        forward = lax.ppermute(forward, axis, right)
        held[peers - step] = forward
        if step < peers - step:
            backward = lax.ppermute(backward, axis, left)
            held[step] = backward
    start = (peers - lax.axis_index(axis)) % peers
    out = []
    for leaf, (dim) in enumerate(dims):
        stacked = jnp.concatenate([held[k][leaf] for k in range(peers)], axis=dim)
        doubled = jnp.concatenate([stacked, stacked], axis=dim)
        size = parts[leaf].shape[dim]
        out.append(lax.dynamic_slice_in_dim(doubled, start * size, peers * size, dim))
    return tuple(out)


def clip_with(weight, largest):
    bound = CLIP_FRACTION * largest
    return jnp.clip(weight.astype(jnp.float32), -bound, bound).astype(jnp.bfloat16)


def column_max(weight):
    return jnp.max(jnp.abs(weight.astype(jnp.float32)), axis=0)


def head_norm(values, head_gain):
    return values * lax.rsqrt(jnp.mean(values * values, axis=-1, keepdims=True) + EPS) * head_gain


def rotate(values, positions):
    half = values.shape[-1] // 2
    freqs = ROPE_BASE ** (-(jnp.arange(half, dtype=jnp.float32) * 2.0 / values.shape[-1]))
    angles = positions.astype(jnp.float32)[:, None] * freqs[None, :]
    cosine = jnp.cos(angles)[:, None, :]
    sine = jnp.sin(angles)[:, None, :]
    first = values[..., :half]
    second = values[..., half:]
    return jnp.concatenate(
        [first * cosine - second * sine, second * cosine + first * sine], axis=-1
    )


def local(tokens, gain, query_gain, key_gain, w_query, w_key, w_value):
    rows = tokens.shape[0]
    query_cols = w_query.shape[1]
    key_cols = w_key.shape[1]
    stacked = jnp.concatenate([w_query, w_key, w_value], axis=1)
    weight_rows, weight_cols = stacked.shape
    aligned = -(-(weight_rows + 1) // TILE_ROWS) * TILE_ROWS
    local_max = jnp.max(jnp.abs(stacked), axis=0)
    padded = jnp.concatenate(
        [
            stacked,
            local_max[None],
            jnp.zeros((aligned - weight_rows - 1, weight_cols), stacked.dtype),
        ],
        axis=0,
    )
    slabs = lax.all_gather(padded, ROW, axis=0, tiled=True).reshape(-1, aligned, weight_cols)
    largest = jnp.max(slabs[:, weight_rows].astype(jnp.float32), axis=0)
    bound = (CLIP_FRACTION * largest).astype(jnp.bfloat16)
    rows_tokens, piece = tokens.shape
    cores = lax.axis_size("cc")
    high = gain.astype(jnp.bfloat16)
    rest = gain - high.astype(jnp.float32)
    middle = rest.astype(jnp.bfloat16)
    low = (rest - middle.astype(jnp.float32)).astype(jnp.bfloat16)
    filler = jnp.zeros((GAIN_ROWS - 3, piece), jnp.bfloat16)
    packed = jnp.concatenate([tokens, high[None], middle[None], low[None], filler], axis=0)
    (along_y,) = ring_gather((packed,), "cy", (1,))
    (along_all,) = ring_gather((along_y,), "cc", (1,))
    blocks = along_all.shape[1] // (cores * piece)
    split = along_all[rows_tokens : rows_tokens + 3].astype(jnp.float32)
    full_gain = split[0] + (split[1] + split[2])
    widened = along_all[:rows_tokens].astype(jnp.float32)
    squares = jnp.sum(widened * widened, axis=1)
    inverse = lax.rsqrt(squares / D + EPS)[:, None]
    whole = (widened * inverse * full_gain[None, :]).astype(jnp.bfloat16)
    ordered = (
        jnp.clip(slabs[:, :weight_rows], -bound, bound)
        .reshape(blocks, cores, piece // weight_rows, weight_rows, weight_cols)
        .transpose(1, 0, 2, 3, 4)
        .reshape(-1, weight_cols)
    )
    kv_part = jnp.dot(whole, ordered[:, query_cols:], preferred_element_type=jnp.float32)
    keys = kv_part[:, :key_cols]
    values = kv_part[:, key_cols:]
    query = jnp.dot(whole, ordered[:, :query_cols], preferred_element_type=jnp.float32)
    heads_local = query_cols // HD
    kv_local = key_cols // HD
    group = heads_local // kv_local
    positions = lax.axis_index(ROW) * rows + jnp.arange(rows, dtype=jnp.int32)
    query = rotate(head_norm(query.reshape(rows, heads_local, HD), query_gain), positions).astype(
        jnp.bfloat16
    )
    keys = rotate(head_norm(keys.reshape(rows, kv_local, HD), key_gain), positions).astype(
        jnp.bfloat16
    )
    values = values.reshape(rows, kv_local, HD).astype(jnp.bfloat16)
    blocks_back = WINDOW // rows
    both = jnp.concatenate([keys, values], axis=1)
    earlier = [shifted(both, ROW, offset) for offset in range(blocks_back, 0, -1)]
    joined = jnp.concatenate(earlier + [both], axis=0)
    all_keys = joined[:, :kv_local]
    all_values = joined[:, kv_local:]
    key_pos = (
        positions[0] - blocks_back * rows + jnp.arange((blocks_back + 1) * rows, dtype=jnp.int32)
    )
    grouped = query.reshape(rows, kv_local, group, HD)
    scores = jnp.einsum(
        "tkgd,skd->kgts", grouped, all_keys, preferred_element_type=jnp.float32
    ) * QUERY_SCALAR ** (-0.5)
    distance = positions[:, None] - key_pos[None, :]
    allowed = (distance >= 0) & (distance < WINDOW) & (key_pos[None, :] >= 0)
    expo = jnp.where(allowed, jnp.exp(scores), 0.0)
    total = jnp.sum(expo, axis=-1, keepdims=True)
    probs = (expo / total).astype(jnp.bfloat16)
    output = jnp.einsum("kgts,skd->tkgd", probs, all_values, preferred_element_type=jnp.float32)
    return output.reshape(rows, query_cols).astype(jnp.bfloat16)


CORES_PER_CHIP = 2
GAIN_ROWS = 8
TILE_ROWS = 16


def solution(mesh):
    rows, cols = mesh.shape["row"], mesh.shape["col"]
    minor = len({tuple(getattr(d, "coords", (0,)))[0] for d in mesh.devices[:, 0].flat})
    if rows % minor:
        minor = 1
    split = Mesh(
        mesh.devices.reshape(rows // minor, minor, cols // CORES_PER_CHIP, CORES_PER_CHIP),
        ("rz", "rx", "cy", "cc"),
    )
    col = ("cy", "cc")
    placed = (
        P(ROW, col),
        P(col),
        P(),
        P(),
        P(ROW, col),
        P(ROW, col),
        P(ROW, col),
    )
    return jax.shard_map(
        local, mesh=split, in_specs=placed, out_specs=P(ROW, col), check_vma=False
    )
```

```python
import jax
import jax.numpy as jnp
from jax import lax
from jax.sharding import Mesh, PartitionSpec as P

D = 5376
HD = 128
WINDOW = 1024


EPS = 1e-06
CLIP_FRACTION = 0.25
QUERY_SCALAR = 168.0
ROPE_BASE = 10000.0


ROW = ("rz", "rx")


def shifted(array, axis, by):
    peers = lax.axis_size(axis)
    pairs = [(i, i + by) for i in range(peers) if 0 <= i + by < peers]
    return lax.ppermute(array, axis, pairs)


def ring_gather(parts, axis, dims):
    peers = lax.axis_size(axis)
    right = [(i, (i + 1) % peers) for i in range(peers)]
    left = [(i, (i - 1) % peers) for i in range(peers)]
    held = {0: parts}
    forward = parts
    backward = parts
    for step in range(1, peers // 2 + 1):
        forward = lax.ppermute(forward, axis, right)
        held[peers - step] = forward
        if step < peers - step:
            backward = lax.ppermute(backward, axis, left)
            held[step] = backward
    start = (peers - lax.axis_index(axis)) % peers
    out = []
    for leaf, (dim) in enumerate(dims):
        stacked = jnp.concatenate([held[k][leaf] for k in range(peers)], axis=dim)
        doubled = jnp.concatenate([stacked, stacked], axis=dim)
        size = parts[leaf].shape[dim]
        out.append(lax.dynamic_slice_in_dim(doubled, start * size, peers * size, dim))
    return tuple(out)


def clip_with(weight, largest):
    bound = CLIP_FRACTION * largest
    return jnp.clip(weight.astype(jnp.float32), -bound, bound).astype(jnp.bfloat16)


def column_max(weight):
    return jnp.max(jnp.abs(weight.astype(jnp.float32)), axis=0)


def head_norm(values, head_gain):
    return values * lax.rsqrt(jnp.mean(values * values, axis=-1, keepdims=True) + EPS) * head_gain


def rotate(values, positions):
    half = values.shape[-1] // 2
    freqs = ROPE_BASE ** (-(jnp.arange(half, dtype=jnp.float32) * 2.0 / values.shape[-1]))
    angles = positions.astype(jnp.float32)[:, None] * freqs[None, :]
    cosine = jnp.cos(angles)[:, None, :]
    sine = jnp.sin(angles)[:, None, :]
    first = values[..., :half]
    second = values[..., half:]
    return jnp.concatenate(
        [first * cosine - second * sine, second * cosine + first * sine], axis=-1
    )


def local(tokens, gain, query_gain, key_gain, w_query, w_key, w_value):
    rows = tokens.shape[0]
    query_cols = w_query.shape[1]
    key_cols = w_key.shape[1]
    stacked = jnp.concatenate([w_query, w_key, w_value], axis=1)
    weight_rows, weight_cols = stacked.shape
    aligned = -(-(weight_rows + 1) // TILE_ROWS) * TILE_ROWS
    local_max = jnp.max(jnp.abs(stacked), axis=0)
    padded = jnp.concatenate(
        [
            stacked,
            local_max[None],
            jnp.zeros((aligned - weight_rows - 1, weight_cols), stacked.dtype),
        ],
        axis=0,
    )
    slabs = lax.all_gather(padded, ROW, axis=0, tiled=True).reshape(-1, aligned, weight_cols)
    largest = jnp.max(slabs[:, weight_rows].astype(jnp.float32), axis=0)

    def clipped_columns(first, last):
        part = slabs[:, :weight_rows, first:last].reshape(-1, last - first)
        return clip_with(part, largest[first:last])

    rows_tokens, piece = tokens.shape
    cores = lax.axis_size("cc")
    high = gain.astype(jnp.bfloat16)
    rest = gain - high.astype(jnp.float32)
    middle = rest.astype(jnp.bfloat16)
    low = (rest - middle.astype(jnp.float32)).astype(jnp.bfloat16)
    filler = jnp.zeros((GAIN_ROWS - 3, piece), jnp.bfloat16)
    packed = jnp.concatenate([tokens, high[None], middle[None], low[None], filler], axis=0)
    (along_y,) = ring_gather((packed,), "cy", (1,))
    (along_all,) = ring_gather((along_y,), "cc", (1,))
    blocks = along_all.shape[1] // (cores * piece)
    split = along_all[rows_tokens : rows_tokens + 3].astype(jnp.float32)
    full_gain = split[0] + (split[1] + split[2])
    widened = along_all[:rows_tokens].astype(jnp.float32)
    squares = jnp.sum(widened * widened, axis=1)
    inverse = lax.rsqrt(squares / D + EPS)[:, None]
    whole = (widened * inverse * full_gain[None, :]).astype(jnp.bfloat16)
    def ordered(first, last):
        part = clipped_columns(first, last)
        return (
            part.reshape(blocks, cores, piece, last - first)
            .transpose(1, 0, 2, 3)
            .reshape(part.shape)
        )

    kv_part = jnp.dot(
        whole, ordered(query_cols, weight_cols), preferred_element_type=jnp.float32
    )
    keys = kv_part[:, :key_cols]
    values = kv_part[:, key_cols:]
    query = jnp.dot(whole, ordered(0, query_cols), preferred_element_type=jnp.float32)
    heads_local = query_cols // HD
    kv_local = key_cols // HD
    group = heads_local // kv_local
    positions = lax.axis_index(ROW) * rows + jnp.arange(rows, dtype=jnp.int32)
    query = rotate(head_norm(query.reshape(rows, heads_local, HD), query_gain), positions).astype(
        jnp.bfloat16
    )
    keys = rotate(head_norm(keys.reshape(rows, kv_local, HD), key_gain), positions).astype(
        jnp.bfloat16
    )
    values = values.reshape(rows, kv_local, HD).astype(jnp.bfloat16)
    blocks_back = WINDOW // rows
    both = jnp.concatenate([keys, values], axis=1).reshape(rows, -1)
    earlier = [shifted(both, ROW, offset) for offset in range(blocks_back, 0, -1)]
    joined = jnp.concatenate(earlier + [both], axis=0).reshape(-1, 2 * kv_local, HD)
    all_keys = joined[:, :kv_local]
    all_values = joined[:, kv_local:]
    key_pos = (
        positions[0] - blocks_back * rows + jnp.arange((blocks_back + 1) * rows, dtype=jnp.int32)
    )
    grouped = query.reshape(rows, kv_local, group, HD)
    scores = jnp.einsum(
        "tkgd,skd->kgts", grouped, all_keys, preferred_element_type=jnp.float32
    ) * QUERY_SCALAR ** (-0.5)
    distance = positions[:, None] - key_pos[None, :]
    allowed = (distance >= 0) & (distance < WINDOW) & (key_pos[None, :] >= 0)
    expo = jnp.where(allowed, jnp.exp(scores), 0.0)
    total = jnp.sum(expo, axis=-1, keepdims=True)
    probs = (expo / total).astype(jnp.bfloat16)
    output = jnp.einsum("kgts,skd->tkgd", probs, all_values, preferred_element_type=jnp.float32)
    return output.reshape(rows, query_cols).astype(jnp.bfloat16)


CORES_PER_CHIP = 2
GAIN_ROWS = 8
TILE_ROWS = 16


def solution(mesh):
    rows, cols = mesh.shape["row"], mesh.shape["col"]
    minor = len({tuple(getattr(d, "coords", (0,)))[0] for d in mesh.devices[:, 0].flat})
    if rows % minor:
        minor = 1
    split = Mesh(
        mesh.devices.reshape(rows // minor, minor, cols // CORES_PER_CHIP, CORES_PER_CHIP),
        ("rz", "rx", "cy", "cc"),
    )
    col = ("cy", "cc")
    placed = (
        P(ROW, col),
        P(col),
        P(),
        P(),
        P(ROW, col),
        P(ROW, col),
        P(ROW, col),
    )
    return jax.shard_map(
        local, mesh=split, in_specs=placed, out_specs=P(ROW, col), check_vma=False
    )
```

```python
import jax
import jax.numpy as jnp
from jax import lax
from jax.sharding import Mesh, PartitionSpec as P

D = 5376
HD = 128
WINDOW = 1024


EPS = 1e-06
CLIP_FRACTION = 0.25
QUERY_SCALAR = 168.0
ROPE_BASE = 10000.0


ROW = ("rz", "rx")


def shifted(array, axis, by):
    peers = lax.axis_size(axis)
    pairs = [(i, i + by) for i in range(peers) if 0 <= i + by < peers]
    return lax.ppermute(array, axis, pairs)


def ring_gather(parts, axis, dims):
    peers = lax.axis_size(axis)
    right = [(i, (i + 1) % peers) for i in range(peers)]
    left = [(i, (i - 1) % peers) for i in range(peers)]
    held = {0: parts}
    forward = parts
    backward = parts
    for step in range(1, peers // 2 + 1):
        forward = lax.ppermute(forward, axis, right)
        held[peers - step] = forward
        if step < peers - step:
            backward = lax.ppermute(backward, axis, left)
            held[step] = backward
    start = (peers - lax.axis_index(axis)) % peers
    out = []
    for leaf, (dim) in enumerate(dims):
        stacked = jnp.concatenate([held[k][leaf] for k in range(peers)], axis=dim)
        doubled = jnp.concatenate([stacked, stacked], axis=dim)
        size = parts[leaf].shape[dim]
        out.append(lax.dynamic_slice_in_dim(doubled, start * size, peers * size, dim))
    return tuple(out)


def clip_with(weight, largest):
    bound = CLIP_FRACTION * largest
    return jnp.clip(weight.astype(jnp.float32), -bound, bound).astype(jnp.bfloat16)


def column_max(weight):
    return jnp.max(jnp.abs(weight.astype(jnp.float32)), axis=0)


def head_norm(values, head_gain):
    return values * lax.rsqrt(jnp.mean(values * values, axis=-1, keepdims=True) + EPS) * head_gain


def rotate(values, positions):
    half = values.shape[-1] // 2
    freqs = ROPE_BASE ** (-(jnp.arange(half, dtype=jnp.float32) * 2.0 / values.shape[-1]))
    angles = positions.astype(jnp.float32)[:, None] * freqs[None, :]
    cosine = jnp.cos(angles)[:, None, :]
    sine = jnp.sin(angles)[:, None, :]
    first = values[..., :half]
    second = values[..., half:]
    return jnp.concatenate(
        [first * cosine - second * sine, second * cosine + first * sine], axis=-1
    )


def local(tokens, gain, query_gain, key_gain, w_query, w_key, w_value):
    rows = tokens.shape[0]
    query_cols = w_query.shape[1]
    key_cols = w_key.shape[1]
    stacked = jnp.concatenate([w_query, w_key, w_value], axis=1)
    weight_rows, weight_cols = stacked.shape
    aligned = -(-(weight_rows + 1) // TILE_ROWS) * TILE_ROWS
    local_max = jnp.max(jnp.abs(stacked), axis=0)
    padded = jnp.concatenate(
        [
            stacked,
            local_max[None],
            jnp.zeros((aligned - weight_rows - 1, weight_cols), stacked.dtype),
        ],
        axis=0,
    )
    slabs = lax.all_gather(padded, ROW, axis=0, tiled=True).reshape(-1, aligned, weight_cols)
    largest = jnp.max(slabs[:, weight_rows].astype(jnp.float32), axis=0)

    def clipped_columns(first, last):
        part = slabs[:, :weight_rows, first:last].reshape(-1, last - first)
        return clip_with(part, largest[first:last])

    rows_tokens, piece = tokens.shape
    cores = lax.axis_size("cc")
    high = gain.astype(jnp.bfloat16)
    rest = gain - high.astype(jnp.float32)
    middle = rest.astype(jnp.bfloat16)
    low = (rest - middle.astype(jnp.float32)).astype(jnp.bfloat16)
    filler = jnp.zeros((GAIN_ROWS - 3, piece), jnp.bfloat16)
    packed = jnp.concatenate([tokens, high[None], middle[None], low[None], filler], axis=0)
    (along_y,) = ring_gather((packed,), "cy", (1,))
    (along_all,) = ring_gather((along_y,), "cc", (1,))
    blocks = along_all.shape[1] // (cores * piece)
    split = along_all[rows_tokens : rows_tokens + 3].astype(jnp.float32)
    full_gain = split[0] + (split[1] + split[2])
    widened = along_all[:rows_tokens].astype(jnp.float32)
    squares = jnp.sum(widened * widened, axis=1)
    inverse = lax.rsqrt(squares / D + EPS)[:, None]
    whole = (widened * inverse * full_gain[None, :]).astype(jnp.bfloat16)
    def ordered(first, last):
        part = clipped_columns(first, last)
        return (
            part.reshape(blocks, cores, piece, last - first)
            .transpose(1, 0, 2, 3)
            .reshape(part.shape)
        )

    kv_part = jnp.dot(
        whole, ordered(query_cols, weight_cols), preferred_element_type=jnp.float32
    )
    keys = kv_part[:, :key_cols]
    values = kv_part[:, key_cols:]
    query = jnp.dot(whole, ordered(0, query_cols), preferred_element_type=jnp.float32)
    heads_local = query_cols // HD
    kv_local = key_cols // HD
    group = heads_local // kv_local
    positions = lax.axis_index(ROW) * rows + jnp.arange(rows, dtype=jnp.int32)
    query = rotate(head_norm(query.reshape(rows, heads_local, HD), query_gain), positions).astype(
        jnp.bfloat16
    )
    keys = rotate(head_norm(keys.reshape(rows, kv_local, HD), key_gain), positions).astype(
        jnp.bfloat16
    )
    values = values.reshape(rows, kv_local, HD).astype(jnp.bfloat16)
    blocks_back = WINDOW // rows
    both = jnp.concatenate([keys, values], axis=1).reshape(rows, -1)
    earlier = [shifted(both, ROW, offset) for offset in range(blocks_back, 0, -1)]
    grouped = query.reshape(rows, kv_local, group, HD)
    parts = []
    for index, block in enumerate(earlier + [both]):
        pair = block.reshape(rows, 2 * kv_local, HD)
        block_keys = pair[:, :kv_local]
        scores = jnp.einsum(
            "tkgd,skd->kgts", grouped, block_keys, preferred_element_type=jnp.float32
        ) * QUERY_SCALAR ** (-0.5)
        key_pos = positions[0] + (index - blocks_back) * rows + jnp.arange(rows, dtype=jnp.int32)
        distance = positions[:, None] - key_pos[None, :]
        allowed = (distance >= 0) & (distance < WINDOW) & (key_pos[None, :] >= 0)
        parts.append((jnp.where(allowed, jnp.exp(scores), 0.0), pair[:, kv_local:]))
    total = sum(jnp.sum(expo, axis=-1, keepdims=True) for expo, _ in parts)
    output = sum(
        jnp.einsum(
            "kgts,skd->tkgd",
            (expo / total).astype(jnp.bfloat16),
            block_values,
            preferred_element_type=jnp.float32,
        )
        for expo, block_values in parts
    )
    return output.reshape(rows, query_cols).astype(jnp.bfloat16)


CORES_PER_CHIP = 2
GAIN_ROWS = 8
TILE_ROWS = 16


def solution(mesh):
    rows, cols = mesh.shape["row"], mesh.shape["col"]
    minor = len({tuple(getattr(d, "coords", (0,)))[0] for d in mesh.devices[:, 0].flat})
    if rows % minor:
        minor = 1
    split = Mesh(
        mesh.devices.reshape(rows // minor, minor, cols // CORES_PER_CHIP, CORES_PER_CHIP),
        ("rz", "rx", "cy", "cc"),
    )
    col = ("cy", "cc")
    placed = (
        P(ROW, col),
        P(col),
        P(),
        P(),
        P(ROW, col),
        P(ROW, col),
        P(ROW, col),
    )
    return jax.shard_map(
        local, mesh=split, in_specs=placed, out_specs=P(ROW, col), check_vma=False
    )
```

```python
import jax
import jax.numpy as jnp
from jax import lax
from jax.sharding import Mesh, PartitionSpec as P

D = 5376
HD = 128
WINDOW = 1024


EPS = 1e-06
CLIP_FRACTION = 0.25
QUERY_SCALAR = 168.0
ROPE_BASE = 10000.0


ROW = ("rz", "rx")


def shifted(array, axis, by):
    peers = lax.axis_size(axis)
    pairs = [(i, i + by) for i in range(peers) if 0 <= i + by < peers]
    return lax.ppermute(array, axis, pairs)


def ring_gather(parts, axis, dims):
    peers = lax.axis_size(axis)
    right = [(i, (i + 1) % peers) for i in range(peers)]
    left = [(i, (i - 1) % peers) for i in range(peers)]
    held = {0: parts}
    forward = parts
    backward = parts
    for step in range(1, peers // 2 + 1):
        forward = lax.ppermute(forward, axis, right)
        held[peers - step] = forward
        if step < peers - step:
            backward = lax.ppermute(backward, axis, left)
            held[step] = backward
    start = (peers - lax.axis_index(axis)) % peers
    out = []
    for leaf, (dim) in enumerate(dims):
        stacked = jnp.concatenate([held[k][leaf] for k in range(peers)], axis=dim)
        doubled = jnp.concatenate([stacked, stacked], axis=dim)
        size = parts[leaf].shape[dim]
        out.append(lax.dynamic_slice_in_dim(doubled, start * size, peers * size, dim))
    return tuple(out)


def clip_with(weight, largest):
    bound = CLIP_FRACTION * largest
    return jnp.clip(weight.astype(jnp.float32), -bound, bound).astype(jnp.bfloat16)


def column_max(weight):
    return jnp.max(jnp.abs(weight.astype(jnp.float32)), axis=0)


def head_norm(values, head_gain):
    return values * lax.rsqrt(jnp.mean(values * values, axis=-1, keepdims=True) + EPS) * head_gain


def rotate(values, positions):
    half = values.shape[-1] // 2
    freqs = ROPE_BASE ** (-(jnp.arange(half, dtype=jnp.float32) * 2.0 / values.shape[-1]))
    angles = positions.astype(jnp.float32)[:, None] * freqs[None, :]
    cosine = jnp.cos(angles)[:, None, :]
    sine = jnp.sin(angles)[:, None, :]
    first = values[..., :half]
    second = values[..., half:]
    return jnp.concatenate(
        [first * cosine - second * sine, second * cosine + first * sine], axis=-1
    )


def local(tokens, gain, query_gain, key_gain, w_query, w_key, w_value):
    rows = tokens.shape[0]
    query_cols = w_query.shape[1]
    key_cols = w_key.shape[1]
    stacked = jnp.concatenate([w_query, w_key, w_value], axis=1)
    weight_rows, weight_cols = stacked.shape
    aligned = -(-(weight_rows + 1) // TILE_ROWS) * TILE_ROWS
    local_max = jnp.max(jnp.abs(stacked), axis=0)
    padded = jnp.concatenate(
        [
            stacked,
            local_max[None],
            jnp.zeros((aligned - weight_rows - 1, weight_cols), stacked.dtype),
        ],
        axis=0,
    )
    slabs = lax.all_gather(padded, ROW, axis=0, tiled=True).reshape(-1, aligned, weight_cols)
    largest = jnp.max(slabs[:, weight_rows].astype(jnp.float32), axis=0)

    def clipped_columns(first, last):
        part = slabs[:, :weight_rows, first:last].reshape(-1, last - first)
        return clip_with(part, largest[first:last])

    rows_tokens, piece = tokens.shape
    cores = lax.axis_size("cc")
    high = gain.astype(jnp.bfloat16)
    rest = gain - high.astype(jnp.float32)
    middle = rest.astype(jnp.bfloat16)
    low = (rest - middle.astype(jnp.float32)).astype(jnp.bfloat16)
    filler = jnp.zeros((GAIN_ROWS - 3, piece), jnp.bfloat16)
    packed = jnp.concatenate([tokens, high[None], middle[None], low[None], filler], axis=0)
    (along_y,) = ring_gather((packed,), "cy", (1,))
    (along_all,) = ring_gather((along_y,), "cc", (1,))
    blocks = along_all.shape[1] // (cores * piece)
    split = along_all[rows_tokens : rows_tokens + 3].astype(jnp.float32)
    full_gain = split[0] + (split[1] + split[2])
    widened = along_all[:rows_tokens].astype(jnp.float32)
    squares = jnp.sum(widened * widened, axis=1)
    inverse = lax.rsqrt(squares / D + EPS)[:, None]
    whole = (widened * inverse * full_gain[None, :]).astype(jnp.bfloat16)
    def ordered(first, last):
        part = clipped_columns(first, last)
        return (
            part.reshape(blocks, cores, piece, last - first)
            .transpose(1, 0, 2, 3)
            .reshape(part.shape)
        )

    kv_part = jnp.dot(
        whole, ordered(query_cols, weight_cols), preferred_element_type=jnp.float32
    )
    keys = kv_part[:, :key_cols]
    values = kv_part[:, key_cols:]
    query = jnp.dot(whole, ordered(0, query_cols), preferred_element_type=jnp.float32)
    heads_local = query_cols // HD
    kv_local = key_cols // HD
    group = heads_local // kv_local
    positions = lax.axis_index(ROW) * rows + jnp.arange(rows, dtype=jnp.int32)
    query = rotate(head_norm(query.reshape(rows, heads_local, HD), query_gain), positions).astype(
        jnp.bfloat16
    )
    keys = rotate(head_norm(keys.reshape(rows, kv_local, HD), key_gain), positions).astype(
        jnp.bfloat16
    )
    values = values.reshape(rows, kv_local, HD).astype(jnp.bfloat16)
    blocks_back = WINDOW // rows
    both = jnp.concatenate([keys, values], axis=1).reshape(rows, -1)
    earlier = [shifted(both, ROW, offset) for offset in range(blocks_back, 0, -1)]
    joined = jnp.concatenate(earlier + [both], axis=0).reshape(-1, 2 * kv_local, HD)
    all_keys = joined[:, :kv_local]
    all_values = joined[:, kv_local:]
    key_pos = (
        positions[0] - blocks_back * rows + jnp.arange((blocks_back + 1) * rows, dtype=jnp.int32)
    )
    grouped = query.reshape(rows, kv_local, group, HD)
    scores = jnp.einsum(
        "tkgd,skd->kgts", grouped, all_keys, preferred_element_type=jnp.float32
    ) * QUERY_SCALAR ** (-0.5)
    distance = positions[:, None] - key_pos[None, :]
    allowed = (distance >= 0) & (distance < WINDOW) & (key_pos[None, :] >= 0)
    expo = jnp.where(allowed, jnp.exp(scores), 0.0)
    total = jnp.sum(expo, axis=-1, keepdims=True)
    probs = (expo * (1.0 / total)).astype(jnp.bfloat16)
    output = jnp.einsum("kgts,skd->tkgd", probs, all_values, preferred_element_type=jnp.float32)
    return output.reshape(rows, query_cols).astype(jnp.bfloat16)


CORES_PER_CHIP = 2
GAIN_ROWS = 8
TILE_ROWS = 16


def solution(mesh):
    rows, cols = mesh.shape["row"], mesh.shape["col"]
    minor = len({tuple(getattr(d, "coords", (0,)))[0] for d in mesh.devices[:, 0].flat})
    if rows % minor:
        minor = 1
    split = Mesh(
        mesh.devices.reshape(rows // minor, minor, cols // CORES_PER_CHIP, CORES_PER_CHIP),
        ("rz", "rx", "cy", "cc"),
    )
    col = ("cy", "cc")
    placed = (
        P(ROW, col),
        P(col),
        P(),
        P(),
        P(ROW, col),
        P(ROW, col),
        P(ROW, col),
    )
    return jax.shard_map(
        local, mesh=split, in_specs=placed, out_specs=P(ROW, col), check_vma=False
    )
```
